128 devices in a mesh: ctx: 16 (over z, x), tp: 8 (over y, core).
Axes of the slice: x: 4, y: 4, z: 4, core: 2. Of those that a mesh axis runs over, the one named last changes fastest.
Arguments:
- tokens: bfloat16 [16384, 4096], P(('ctx', 'tp')), may hold values from -21 to 21
- segment: int32 [16384], P('ctx'), may hold values from 0 to 3, never falling along the last dimension, each value on 1 to 8704 neighbouring positions
- w_feat_q: bfloat16 [4096, 512], P(None, 'tp'), may hold values from -0.09375 to 0.09375
- w_feat_k: bfloat16 [4096, 512], P(None, 'tp'), may hold values from -0.09375 to 0.09375
- w_query: bfloat16 [4096, 4096], P(None, 'tp'), may hold values from -0.09375 to 0.09375
- w_key: bfloat16 [4096, 4096], P(None, 'tp'), may hold values from -0.09375 to 0.09375
- w_value: bfloat16 [4096, 4096], P(None, 'tp'), may hold values from -0.09375 to 0.09375
- w_out: bfloat16 [4096, 4096], P('tp'), may hold values from -0.09375 to 0.09375
Outputs:
- layer_out: bfloat16 [16384, 4096], P(('ctx', 'tp'))
The draws below stay inside these ranges and needn't reach their ends.
Inputs may be any that keep to these rules, and one draw needn't show every extreme that they name: `segment`: never falls along the sequence; 4 documents, each of 1 to 8704 tokens, one of exactly 8704.
All inputs are finite; a program needn't handle non-finite values.
Results may differ from the reference program's by a relative error of at most 0.006.
The reference program's roundings to bfloat16 on the way (of `mixed`) count: a program that leaves them out, or rounds other values in their place, can miss the bound.
Values may be sent and summed in bfloat16 or wider, within the bound.
No kernel may reach another device: no remote copies, remote signals or barrier semaphores. Data moves between devices by JAX's collectives and lax.ppermute only.
A program may use at most 128 MiB of HBM per device.

```python
import math
import jax
import jax.numpy as jnp
import numpy as np
from jax import lax

D = 4096
HEADS = 32
HEAD_DIM = 128
FEAT = 16
WINDOW = 64
TOK_DEV = 1024
TAYLOR = 273
TOKENS = 16384
DOCS = 4
DOC_MOST = 8704


def draw_tokens(key, part):
    key_value = jax.random.fold_in(key, 1)
    values = jnp.clip(jax.random.normal(key_value, (TOKENS, D), jnp.float32), -6.0, 6.0)
    return values.astype(jnp.bfloat16)


def block_scale(stream_key, shape, shards, low, largest):
    factor_of, own = 1.0, jax.random.fold_in(stream_key, 6)
    for dim, shards_of in shards:
        draws = jnp.exp(jax.random.uniform(jax.random.fold_in(own, dim), (shards_of,), jnp.float32, low / len(shards), largest / len(shards)))
        factor_of = factor_of * jnp.repeat(draws, shape[dim] // shards_of).reshape([-1 if axis == dim else 1 for axis in range(len(shape))])
    return factor_of


def split_up(amount, total, reach, lean):
    loads = [(1 << 20) // math.isqrt(standing ** lean) + 1 for standing in range(2, amount + 1)]
    spare, given = total - reach - (amount - 1), [1] * (amount - 1)
    while spare > 0:
        movable = [i for i in range(amount - 1) if given[i] < reach]
        pool, budget = sum([loads[i] for i in movable]), spare
        for i in movable:
            addition = min(reach - given[i], max(1, budget * loads[i] // pool), spare)
            given[i] = given[i] + addition
            spare = spare - addition
    return np.array([reach] + given)


def ragged(rng, count, total, reach, skew):
    if count == 2:
        one = jax.random.randint(rng, (), max(1, total - reach), min(reach, total - 1) + 1)
        return jnp.stack([one, total - one])
    tallies = jnp.asarray(split_up(count, total, reach, skew), jnp.int32)
    pairs = (count - 1) // 2
    source_of, sink = tallies[1:1 + 2 * pairs:2], tallies[2:2 + 2 * pairs:2]
    slack = jnp.minimum(source_of - 1, reach - sink)
    shifted = jax.random.randint(jax.random.fold_in(rng, 1), (pairs,), 0, 1 << 20) % (slack + 1)
    tallies = tallies.at[1:1 + 2 * pairs:2].set(source_of - shifted).at[2:2 + 2 * pairs:2].set(sink + shifted)
    return tallies[jax.random.permutation(jax.random.fold_in(rng, 2), count)]


def normal_values(own_key, dims, scale, reach, pieces=(), kind=jnp.bfloat16):
    values = jax.random.normal(own_key, dims, jnp.float32) * scale
    if len(pieces) > 0:
        values = block_scale(own_key, dims, pieces, -0.22, 0.18) * values
    return jnp.clip(values, min=-reach, max=reach).astype(kind)


def setup_inputs(seed: int = 0) -> dict:
    key_list = jax.random.split(jax.random.key(seed), 9)
    return {
        "tokens": draw_tokens(jax.random.fold_in(key_list[8], 71), 0),
        "segment": jnp.searchsorted(jnp.cumsum(ragged(key_list[1], DOCS, TOKENS, DOC_MOST, 1)), jnp.arange(TOKENS), side="right").astype(jnp.int32),
        "w_feat_q": normal_values(key_list[2], (D, HEADS * FEAT), D ** -0.5, 0.09375, ((1, 8),)),
        "w_feat_k": normal_values(key_list[3], (D, HEADS * FEAT), D ** -0.5, 0.09375, ((1, 8),)),
        "w_query": normal_values(key_list[4], (D, HEADS * HEAD_DIM), D ** -0.5, 0.09375, ((1, 8),)),
        "w_key": normal_values(key_list[5], (D, HEADS * HEAD_DIM), D ** -0.5, 0.09375, ((1, 8),)),
        "w_value": normal_values(key_list[6], (D, HEADS * HEAD_DIM), D ** -0.5, 0.09375, ((1, 8),)),
        "w_out": normal_values(key_list[7], (HEADS * HEAD_DIM, D), (HEADS * HEAD_DIM) ** -0.5, 0.09375, ((0, 8),)),
    }


HIGH = lax.Precision.HIGHEST


def taylor_map(values):
    width = values.shape[-1]
    square = (values[..., :, None] * values[..., None, :]).reshape(values.shape[:-1] + (width * width,))
    ones = jnp.ones(values.shape[:-1] + (1,), values.dtype)
    return jnp.concatenate([ones, values * width ** -0.25, square * (0.5 ** 0.5 / width ** 0.5)], axis=-1)


def heads_of(tokens, weight, width):
    total = tokens.shape[0]
    projected = jnp.dot(tokens, weight, preferred_element_type=jnp.float32).astype(jnp.bfloat16)
    projected = lax.optimization_barrier(projected)
    return projected.astype(jnp.float32).reshape(total, -1, width).transpose(1, 0, 2)


def reference(tokens, segment, w_feat_q, w_feat_k, w_query, w_key, w_value, w_out):
    feat_q = heads_of(tokens, w_feat_q, FEAT)
    feat_k = heads_of(tokens, w_feat_k, FEAT)
    query_w = heads_of(tokens, w_query, HEAD_DIM)
    key_w = heads_of(tokens, w_key, HEAD_DIM)
    value = heads_of(tokens, w_value, HEAD_DIM)
    block = min(512, TOK_DEV)
    count = TOKENS // block

    def blocked(array):
        return array.reshape(HEADS, count, block, array.shape[-1]).transpose(1, 0, 2, 3)

    seg_blocks = segment.reshape(count, block)
    init = (jnp.zeros((HEADS, TAYLOR, HEAD_DIM), jnp.float32), jnp.zeros((HEADS, TAYLOR), jnp.float32),
            jnp.array(-1, jnp.int32), jnp.zeros((HEADS, WINDOW, HEAD_DIM), jnp.float32),
            jnp.zeros((HEADS, WINDOW, HEAD_DIM), jnp.float32), jnp.full((WINDOW,), -1, jnp.int32))

    def advance(carry, inputs):
        state, normal, last_seg, tail_key, tail_value, tail_seg = carry
        query_f, key_f, query_n, key_n, values, seg = inputs
        rows = jnp.arange(block)
        allowed = (seg[:, None] == seg[None, :]) & (rows[None, :] <= rows[:, None])
        inner = jnp.einsum('hsf,htf->hst', query_f, key_f, precision=HIGH) / FEAT ** 0.5
        kernel = jnp.where(allowed[None], 1.0 + inner + 0.5 * inner * inner, 0.0)
        numerator = jnp.einsum('hst,htd->hsd', kernel, values, precision=HIGH)
        denominator = jnp.sum(kernel, axis=-1)
        mapped_q = taylor_map(query_f)
        carried = (seg == last_seg)[None, :]
        numerator = numerator + jnp.where(carried[..., None], jnp.einsum('hsf,hfd->hsd', mapped_q, state, precision=HIGH), 0.0)
        denominator = denominator + jnp.where(carried, jnp.einsum('hsf,hf->hs', mapped_q, normal, precision=HIGH), 0.0)
        linear_part = numerator / denominator[..., None]
        key_rows = jnp.concatenate([tail_key, key_n], axis=1)
        value_rows = jnp.concatenate([tail_value, values], axis=1)
        key_seg = jnp.concatenate([tail_seg, seg])
        columns = jnp.arange(WINDOW + block)
        near = (columns[None, :] <= rows[:, None] + WINDOW) & (columns[None, :] > rows[:, None])
        visible = near & (key_seg[None, :] == seg[:, None])
        scores = jnp.einsum('hsd,htd->hst', query_n, key_rows, precision=HIGH) / HEAD_DIM ** 0.5
        scores = jnp.where(visible[None], scores, -jnp.inf)
        peak = jnp.max(scores, axis=-1, keepdims=True)
        expo = jnp.exp(scores - peak)
        window_part = jnp.einsum('hst,htd->hsd', expo, value_rows, precision=HIGH) / jnp.sum(expo, axis=-1)[..., None]
        mixed = (linear_part + window_part).astype(jnp.bfloat16)
        mapped_k = taylor_map(key_f) * (seg == seg[-1])[None, :, None].astype(jnp.float32)
        tail_state = jnp.einsum('htf,htd->hfd', mapped_k, values, precision=HIGH)
        tail_normal = jnp.sum(mapped_k, axis=1)
        keep = (seg[0] == seg[-1]) & (last_seg == seg[-1])
        state = tail_state + jnp.where(keep, state, 0.0)
        normal = tail_normal + jnp.where(keep, normal, 0.0)
        new_carry = (state, normal, seg[-1], key_rows[:, -WINDOW:], value_rows[:, -WINDOW:], key_seg[-WINDOW:])
        return new_carry, mixed

    final, mixed = lax.scan(advance, init, (blocked(feat_q), blocked(feat_k), blocked(query_w), blocked(key_w), blocked(value), seg_blocks))
    mixed = mixed.transpose(0, 2, 1, 3).reshape(TOKENS, HEADS * HEAD_DIM)
    return jnp.dot(mixed, w_out, preferred_element_type=jnp.float32).astype(jnp.bfloat16)
```

```python
import jax
import jax.numpy as jnp
from jax import lax
from jax.sharding import PartitionSpec as P

HEAD_DIM = 128
FEAT = 16
WINDOW = 64


HIGH = lax.Precision.HIGHEST


def passed_along(block, axis, distance):
    devices = range(lax.axis_size(axis))
    route = [(i - distance, i) for i in devices if i - distance in devices]
    return lax.ppermute(block, axis, route)


def carried_in(state, normal, last, axis):
    place = lax.axis_index(axis)
    length = lax.axis_size(axis)
    distance = 1
    while distance < length:
        early_state, early_normal, early_last = passed_along((state, normal, last), axis, distance)
        absorb = (place >= distance) & (early_last == last)
        state = state + jnp.where(absorb, early_state, 0.0)
        normal = normal + jnp.where(absorb, early_normal, 0.0)
        distance *= 2
    early_state, early_normal, early_last = passed_along((state, normal, last), axis, 1)
    reached = place >= 1
    return (
        jnp.where(reached, early_state, 0.0),
        jnp.where(reached, early_normal, 0.0),
        jnp.where(reached, early_last, -1),
    )


def taylor_map(values):
    width = values.shape[-1]
    square = (values[..., :, None] * values[..., None, :]).reshape(
        values.shape[:-1] + (width * width,)
    )
    ones = jnp.ones(values.shape[:-1] + (1,), values.dtype)
    return jnp.concatenate(
        [ones, values * width ** (-0.25), square * (0.5**0.5 / width**0.5)], axis=-1
    )


def heads_split(flat, width):
    return flat.reshape(flat.shape[0], -1, width).transpose(1, 0, 2)


def body(tokens, segment, w_feat_q, w_feat_k, w_query, w_key, w_value, w_out):
    weights = (w_feat_q, w_feat_k, w_query, w_key, w_value)
    piece = lax.all_gather(tokens, "tp", axis=0, tiled=True)
    joined_bf = jnp.concatenate(
        [
            jnp.dot(piece, weight, preferred_element_type=jnp.float32).astype(jnp.bfloat16)
            for weight in weights
        ],
        axis=1,
    )
    joined = lax.optimization_barrier(joined_bf).astype(jnp.float32)
    feat_width = w_feat_q.shape[1]
    head_width = w_query.shape[1]
    offset_w = 2 * feat_width
    feat_q = heads_split(joined[:, :feat_width], FEAT)
    feat_k = heads_split(joined[:, feat_width:offset_w], FEAT)
    value = heads_split(joined[:, offset_w + 2 * head_width :], HEAD_DIM)
    feat_q_bf = heads_split(joined_bf[:, :feat_width], FEAT)
    feat_k_bf = heads_split(joined_bf[:, feat_width:offset_w], FEAT)
    query_bf = heads_split(joined_bf[:, offset_w : offset_w + head_width], HEAD_DIM)
    key_all_bf = heads_split(
        joined_bf[:, offset_w + head_width : offset_w + 2 * head_width], HEAD_DIM
    )
    rows_here = segment.shape[0]
    key_tail_bf = key_all_bf[:, -WINDOW:]
    value_tail_bf = heads_split(joined_bf[-WINDOW:, offset_w + 2 * head_width :], HEAD_DIM)
    seg_mark = (segment[-WINDOW:] + 1).astype(jnp.bfloat16)
    tail_key, tail_value, tail_mark = passed_along((key_tail_bf, value_tail_bf, seg_mark), "ctx", 1)
    mapped_k = taylor_map(feat_k) * (segment == segment[-1])[None, :, None].astype(jnp.float32)
    own_state = jnp.einsum("htf,htd->hfd", mapped_k, value, precision=HIGH)
    own_normal = jnp.sum(mapped_k, axis=1)
    carried_state, carried_normal, carried_last = carried_in(
        own_state, own_normal, segment[-1:], "ctx"
    )
    seg_float = segment.astype(jnp.float32)
    key_rows = jnp.concatenate([tail_key, key_all_bf], axis=1)
    value_rows = jnp.concatenate([tail_value.astype(jnp.float32), value], axis=1)
    key_seg = jnp.concatenate([tail_mark.astype(jnp.float32), seg_float + 1.0])
    block = min(512, rows_here)
    results = []
    for begin in range(0, rows_here, block):
        finish = begin + block
        query_pos = jnp.arange(begin, finish)
        key_pos = jnp.arange(finish)
        seg_here = seg_float[begin:finish]
        allowed = (seg_here[:, None] == seg_float[None, :finish]) & (
            key_pos[None, :] <= query_pos[:, None]
        )
        inner = (
            jnp.einsum(
                "hsf,htf->hst",
                feat_q_bf[:, begin:finish],
                feat_k_bf[:, :finish],
                preferred_element_type=jnp.float32,
            )
            / FEAT**0.5
        )
        kernel = jnp.where(allowed[None], 1.0 + inner + 0.5 * inner * inner, 0.0)
        numerator = jnp.einsum("hst,htd->hsd", kernel, value[:, :finish], precision=HIGH)
        denominator = jnp.sum(kernel, axis=-1)
        mapped_q = taylor_map(feat_q[:, begin:finish])
        carried = (seg_here == carried_last.astype(jnp.float32))[None, :]
        numerator = numerator + jnp.where(
            carried[..., None],
            jnp.einsum("hsf,hfd->hsd", mapped_q, carried_state, precision=HIGH),
            0.0,
        )
        denominator = denominator + jnp.where(
            carried, jnp.einsum("hsf,hf->hs", mapped_q, carried_normal, precision=HIGH), 0.0
        )
        linear_part = numerator / denominator[..., None]
        columns = jnp.arange(begin, finish + WINDOW)
        near = (columns[None, :] <= query_pos[:, None] + WINDOW) & (
            columns[None, :] > query_pos[:, None]
        )
        visible = near & (key_seg[begin : finish + WINDOW][None, :] == seg_here[:, None] + 1.0)
        scores = (
            jnp.einsum(
                "hsd,htd->hst",
                query_bf[:, begin:finish],
                key_rows[:, begin : finish + WINDOW],
                preferred_element_type=jnp.float32,
            )
            / HEAD_DIM**0.5
        )
        scores = jnp.where(visible[None], scores, -jnp.inf)
        peak = jnp.max(scores, axis=-1, keepdims=True)
        expo = jnp.exp(scores - peak)
        window_part = (
            jnp.einsum("hst,htd->hsd", expo, value_rows[:, begin : finish + WINDOW], precision=HIGH)
            / jnp.sum(expo, axis=-1)[..., None]
        )
        results.append(linear_part + window_part)
    mixed = (
        jnp.concatenate(results, axis=1)
        .transpose(1, 0, 2)
        .reshape(rows_here, head_width)
        .astype(jnp.bfloat16)
    )
    return lax.psum_scatter(
        jnp.dot(mixed, w_out, preferred_element_type=jnp.float32),
        "tp",
        scatter_dimension=0,
        tiled=True,
    ).astype(jnp.bfloat16)


def solution(mesh):
    in_specs = (
        P(("ctx", "tp"), None),
        P("ctx"),
        P(None, "tp"),
        P(None, "tp"),
        P(None, "tp"),
        P(None, "tp"),
        P(None, "tp"),
        P("tp", None),
    )
    out_specs = P(("ctx", "tp"), None)
    return jax.shard_map(body, mesh=mesh, in_specs=in_specs, out_specs=out_specs, check_vma=False)
```

```python
import jax
import jax.numpy as jnp
from jax import lax
from jax.sharding import PartitionSpec as P

HEAD_DIM = 128
FEAT = 16
WINDOW = 64


HIGH = lax.Precision.HIGH


def passed_along(block, axis, distance):
    devices = range(lax.axis_size(axis))
    route = [(i - distance, i) for i in devices if i - distance in devices]
    return lax.ppermute(block, axis, route)


def carried_in(state, normal, last, axis):
    place = lax.axis_index(axis)
    length = lax.axis_size(axis)
    heads, features, width = state.shape
    extra = -(-(features + 1) // width)
    tagged = jnp.concatenate(
        [normal, jnp.broadcast_to(last.astype(jnp.float32), (heads, 1))], axis=1
    )
    tagged = jnp.pad(tagged, ((0, 0), (0, extra * width - features - 1)))
    packed = jnp.concatenate([state, tagged.reshape(heads, extra, width)], axis=1)
    tag = last.astype(jnp.float32)[0]
    distance = 1
    while distance < length:
        early = passed_along(packed, axis, distance)
        early_tag = early[0, features + features // width, features % width]
        absorb = (place >= distance) & (early_tag == tag)
        packed = packed + jnp.where(absorb, early, 0.0)
        packed = packed.at[:, features + features // width, features % width].set(tag)
        distance *= 2
    early = passed_along(packed, axis, 1)
    reached = place >= 1
    early = jnp.where(reached, early, 0.0)
    flat = early[:, features:].reshape(heads, extra * width)
    early_tag = jnp.where(reached, flat[0, features], -1.0)
    return early[:, :features], flat[:, :features], early_tag


def taylor_map(values):
    width = values.shape[-1]
    square = (values[..., :, None] * values[..., None, :]).reshape(
        values.shape[:-1] + (width * width,)
    )
    ones = jnp.ones(values.shape[:-1] + (1,), values.dtype)
    return jnp.concatenate(
        [ones, values * width ** (-0.25), square * (0.5**0.5 / width**0.5)], axis=-1
    )


def heads_split(flat, width):
    return flat.reshape(flat.shape[0], -1, width).transpose(1, 0, 2)


def body(tokens, segment, w_feat_q, w_feat_k, w_query, w_key, w_value, w_out):
    weights = (w_feat_q, w_feat_k, w_query, w_key, w_value)
    piece = lax.all_gather(tokens, "tp", axis=0, tiled=True)
    joined_bf = jnp.concatenate(
        [
            jnp.dot(piece, weight, preferred_element_type=jnp.float32).astype(jnp.bfloat16)
            for weight in weights
        ],
        axis=1,
    )
    joined = lax.optimization_barrier(joined_bf).astype(jnp.float32)
    feat_width = w_feat_q.shape[1]
    head_width = w_query.shape[1]
    offset_w = 2 * feat_width
    feat_q = heads_split(joined[:, :feat_width], FEAT)
    feat_k = heads_split(joined[:, feat_width:offset_w], FEAT)
    value = heads_split(joined[:, offset_w + 2 * head_width :], HEAD_DIM)
    feat_q_bf = heads_split(joined_bf[:, :feat_width], FEAT)
    feat_k_bf = heads_split(joined_bf[:, feat_width:offset_w], FEAT)
    query_bf = heads_split(joined_bf[:, offset_w : offset_w + head_width], HEAD_DIM)
    key_all_bf = heads_split(
        joined_bf[:, offset_w + head_width : offset_w + 2 * head_width], HEAD_DIM
    )
    rows_here = segment.shape[0]
    key_tail_bf = key_all_bf[:, -WINDOW:]
    value_tail_bf = heads_split(joined_bf[-WINDOW:, offset_w + 2 * head_width :], HEAD_DIM)
    seg_mark = (segment[-WINDOW:] + 1).astype(jnp.bfloat16)
    tail_key, tail_value, tail_mark = passed_along((key_tail_bf, value_tail_bf, seg_mark), "ctx", 1)
    mapped_k = taylor_map(feat_k) * (segment == segment[-1])[None, :, None].astype(jnp.float32)
    own_state = jnp.einsum("htf,htd->hfd", mapped_k, value, precision=HIGH)
    own_normal = jnp.sum(mapped_k, axis=1)
    carried_state, carried_normal, carried_last = carried_in(
        own_state, own_normal, segment[-1:], "ctx"
    )
    seg_float = segment.astype(jnp.float32)
    key_rows = jnp.concatenate([tail_key, key_all_bf], axis=1)
    value_rows = jnp.concatenate([tail_value.astype(jnp.float32), value], axis=1)
    key_seg = jnp.concatenate([tail_mark.astype(jnp.float32), seg_float + 1.0])
    block = min(512, rows_here)
    results = []
    for begin in range(0, rows_here, block):
        finish = begin + block
        query_pos = jnp.arange(begin, finish)
        key_pos = jnp.arange(finish)
        seg_here = seg_float[begin:finish]
        allowed = (seg_here[:, None] == seg_float[None, :finish]) & (
            key_pos[None, :] <= query_pos[:, None]
        )
        inner = (
            jnp.einsum(
                "hsf,htf->hst",
                feat_q_bf[:, begin:finish],
                feat_k_bf[:, :finish],
                preferred_element_type=jnp.float32,
            )
            / FEAT**0.5
        )
        kernel = jnp.where(allowed[None], 1.0 + inner + 0.5 * inner * inner, 0.0)
        numerator = jnp.einsum("hst,htd->hsd", kernel, value[:, :finish], precision=HIGH)
        denominator = jnp.sum(kernel, axis=-1)
        mapped_q = taylor_map(feat_q[:, begin:finish])
        carried = (seg_here == carried_last)[None, :]
        numerator = numerator + jnp.where(
            carried[..., None],
            jnp.einsum("hsf,hfd->hsd", mapped_q, carried_state, precision=HIGH),
            0.0,
        )
        denominator = denominator + jnp.where(
            carried, jnp.einsum("hsf,hf->hs", mapped_q, carried_normal, precision=HIGH), 0.0
        )
        linear_part = numerator / denominator[..., None]
        columns = jnp.arange(begin, finish + WINDOW)
        near = (columns[None, :] <= query_pos[:, None] + WINDOW) & (
            columns[None, :] > query_pos[:, None]
        )
        visible = near & (key_seg[begin : finish + WINDOW][None, :] == seg_here[:, None] + 1.0)
        scores = (
            jnp.einsum(
                "hsd,htd->hst",
                query_bf[:, begin:finish],
                key_rows[:, begin : finish + WINDOW],
                preferred_element_type=jnp.float32,
            )
            / HEAD_DIM**0.5
        )
        scores = jnp.where(visible[None], scores, -jnp.inf)
        peak = jnp.max(scores, axis=-1, keepdims=True)
        expo = jnp.exp(scores - peak)
        window_part = (
            jnp.einsum("hst,htd->hsd", expo, value_rows[:, begin : finish + WINDOW], precision=HIGH)
            / jnp.sum(expo, axis=-1)[..., None]
        )
        results.append(linear_part + window_part)
    mixed = (
        jnp.concatenate(results, axis=1)
        .transpose(1, 0, 2)
        .reshape(rows_here, head_width)
        .astype(jnp.bfloat16)
    )
    return lax.psum_scatter(
        jnp.dot(mixed, w_out, preferred_element_type=jnp.float32).astype(jnp.bfloat16),
        "tp",
        scatter_dimension=0,
        tiled=True,
    )


def solution(mesh):
    in_specs = (
        P(("ctx", "tp"), None),
        P("ctx"),
        P(None, "tp"),
        P(None, "tp"),
        P(None, "tp"),
        P(None, "tp"),
        P(None, "tp"),
        P("tp", None),
    )
    out_specs = P(("ctx", "tp"), None)
    return jax.shard_map(body, mesh=mesh, in_specs=in_specs, out_specs=out_specs, check_vma=False)
```

```python
import jax
import numpy as np
import jax.numpy as jnp
from jax import lax
from jax.sharding import PartitionSpec as P

HEAD_DIM = 128
FEAT = 16
WINDOW = 64


HIGH = lax.Precision.HIGH


def passed_along(block, axis, distance):
    devices = range(lax.axis_size(axis))
    route = [(i - distance, i) for i in devices if i - distance in devices]
    return lax.ppermute(block, axis, route)


def carried_in(state, normal, last, axis):
    place = lax.axis_index(axis)
    length = lax.axis_size(axis)
    heads, features, width = state.shape
    extra = -(-(features + 1) // width)
    tagged = jnp.concatenate(
        [normal, jnp.broadcast_to(last.astype(jnp.float32), (heads, 1))], axis=1
    )
    tagged = jnp.pad(tagged, ((0, 0), (0, extra * width - features - 1)))
    packed = jnp.concatenate([state, tagged.reshape(heads, extra, width)], axis=1)
    tag = last.astype(jnp.float32)[0]
    distance = 1
    while distance < length:
        early = passed_along(packed, axis, distance)
        early_tag = early[0, features + features // width, features % width]
        absorb = (place >= distance) & (early_tag == tag)
        packed = packed + jnp.where(absorb, early, 0.0)
        packed = packed.at[:, features + features // width, features % width].set(tag)
        distance *= 2
    early = passed_along(packed, axis, 1)
    reached = place >= 1
    early = jnp.where(reached, early, 0.0)
    flat = early[:, features:].reshape(heads, extra * width)
    early_tag = jnp.where(reached, flat[0, features], -1.0)
    return early[:, :features], flat[:, :features], early_tag


def taylor_map(values):
    width = values.shape[-1]
    square = (values[..., :, None] * values[..., None, :]).reshape(
        values.shape[:-1] + (width * width,)
    )
    ones = jnp.ones(values.shape[:-1] + (1,), values.dtype)
    return jnp.concatenate(
        [ones, values * width ** (-0.25), square * (0.5**0.5 / width**0.5)], axis=-1
    )


def heads_split(flat, width):
    return flat.reshape(flat.shape[0], -1, width).transpose(1, 0, 2)


def body(tokens, segment, w_feat_q, w_feat_k, w_query, w_key, w_value, w_out):
    weights = (w_feat_q, w_feat_k, w_query, w_key, w_value)
    piece = lax.all_gather(tokens, "tp", axis=0, tiled=True)
    joined_bf = jnp.concatenate(
        [
            jnp.dot(piece, weight, preferred_element_type=jnp.float32).astype(jnp.bfloat16)
            for weight in weights
        ],
        axis=1,
    )
    joined = lax.optimization_barrier(joined_bf).astype(jnp.float32)
    feat_width = w_feat_q.shape[1]
    head_width = w_query.shape[1]
    offset_w = 2 * feat_width
    feat_q = heads_split(joined[:, :feat_width], FEAT)
    feat_k = heads_split(joined[:, feat_width:offset_w], FEAT)
    value = heads_split(joined[:, offset_w + 2 * head_width :], HEAD_DIM)
    feat_q_bf = heads_split(joined_bf[:, :feat_width], FEAT)
    feat_k_bf = heads_split(joined_bf[:, feat_width:offset_w], FEAT)
    query_bf = heads_split(joined_bf[:, offset_w : offset_w + head_width], HEAD_DIM)
    key_all_bf = heads_split(
        joined_bf[:, offset_w + head_width : offset_w + 2 * head_width], HEAD_DIM
    )
    rows_here = segment.shape[0]
    key_tail_bf = key_all_bf[:, -WINDOW:]
    value_tail_bf = heads_split(joined_bf[-WINDOW:, offset_w + 2 * head_width :], HEAD_DIM)
    seg_mark = (segment[-WINDOW:] + 1).astype(jnp.bfloat16)
    tail_key, tail_value, tail_mark = passed_along((key_tail_bf, value_tail_bf, seg_mark), "ctx", 1)
    mapped_k = taylor_map(feat_k) * (segment == segment[-1])[None, :, None].astype(jnp.float32)
    own_state = jnp.einsum("htf,htd->hfd", mapped_k, value, precision=HIGH)
    own_normal = jnp.sum(mapped_k, axis=1)
    carried_state, carried_normal, carried_last = carried_in(
        own_state, own_normal, segment[-1:], "ctx"
    )
    seg_float = segment.astype(jnp.float32)
    key_rows = jnp.concatenate([tail_key, key_all_bf], axis=1)
    value_rows = jnp.concatenate([tail_value.astype(jnp.float32), value], axis=1)
    key_seg = jnp.concatenate([tail_mark.astype(jnp.float32), seg_float + 1.0])
    owners = lax.axis_size("tp")
    own = rows_here // owners
    chunks = 2
    sub = own // chunks
    heads = feat_q.shape[0]

    def pick(array, j):
        shape = array.shape
        grouped = array.reshape(shape[:-2] + (owners, own, shape[-1]))
        return grouped[..., sub * j : sub * (j + 1), :].reshape(shape[:-2] + (owners * sub, shape[-1]))

    local = np.arange(sub)
    reach = np.arange(sub + WINDOW)
    near = (reach[None, :] <= local[:, None] + WINDOW) & (reach[None, :] > local[:, None])
    pieces = []
    for j in range(chunks):
        query_pos = (np.arange(owners)[:, None] * own + sub * j + local[None, :]).reshape(-1)
        key_pos = np.arange(rows_here)
        seg_here = seg_float.reshape(owners, own)[:, sub * j : sub * (j + 1)].reshape(-1)
        allowed = (seg_here[:, None] == seg_float[None, :]) & (key_pos[None, :] <= query_pos[:, None])
        inner = (
            jnp.einsum(
                "hsf,htf->hst",
                pick(feat_q_bf, j),
                feat_k_bf,
                preferred_element_type=jnp.float32,
            )
            / FEAT**0.5
        )
        kernel = jnp.where(allowed[None], 1.0 + inner + 0.5 * inner * inner, 0.0)
        numerator = jnp.einsum("hst,htd->hsd", kernel, value, precision=HIGH)
        denominator = jnp.sum(kernel, axis=-1)
        mapped_q = taylor_map(pick(feat_q, j))
        carried = (seg_here == carried_last)[None, :]
        numerator = numerator + jnp.where(
            carried[..., None],
            jnp.einsum("hsf,hfd->hsd", mapped_q, carried_state, precision=HIGH),
            0.0,
        )
        denominator = denominator + jnp.where(
            carried, jnp.einsum("hsf,hf->hs", mapped_q, carried_normal, precision=HIGH), 0.0
        )
        linear_part = numerator / denominator[..., None]
        starts = [b * own + sub * j for b in range(owners)]
        key_blocks = jnp.stack([key_rows[:, s : s + sub + WINDOW] for s in starts], axis=1)
        value_blocks = jnp.stack([value_rows[:, s : s + sub + WINDOW] for s in starts], axis=1)
        seg_blocks = jnp.stack([key_seg[s : s + sub + WINDOW] for s in starts], axis=0)
        query_blocks = pick(query_bf, j).reshape(heads, owners, sub, HEAD_DIM)
        visible = near[None] & (seg_blocks[:, None, :] == seg_here.reshape(owners, sub)[:, :, None] + 1.0)
        scores = (
            jnp.einsum(
                "hbsd,hbtd->hbst",
                query_blocks,
                key_blocks,
                preferred_element_type=jnp.float32,
            )
            / HEAD_DIM**0.5
        )
        scores = jnp.where(visible[None], scores, -jnp.inf)
        peak = jnp.max(scores, axis=-1, keepdims=True)
        expo = jnp.exp(scores - peak)
        window_part = (
            jnp.einsum("hbst,hbtd->hbsd", expo, value_blocks, precision=HIGH)
            / jnp.sum(expo, axis=-1)[..., None]
        ).reshape(heads, owners * sub, HEAD_DIM)
        mixed = (
            (linear_part + window_part)
            .transpose(1, 0, 2)
            .reshape(owners * sub, head_width)
            .astype(jnp.bfloat16)
        )
        pieces.append(
            lax.psum_scatter(
                jnp.dot(mixed, w_out, preferred_element_type=jnp.float32),
                "tp",
                scatter_dimension=0,
                tiled=True,
            ).astype(jnp.bfloat16)
        )
    return jnp.concatenate(pieces, axis=0)


def solution(mesh):
    in_specs = (
        P(("ctx", "tp"), None),
        P("ctx"),
        P(None, "tp"),
        P(None, "tp"),
        P(None, "tp"),
        P(None, "tp"),
        P(None, "tp"),
        P("tp", None),
    )
    out_specs = P(("ctx", "tp"), None)
    return jax.shard_map(body, mesh=mesh, in_specs=in_specs, out_specs=out_specs, check_vma=False)
```

```python
import jax
import numpy as np
import jax.numpy as jnp
from jax import lax
from jax.sharding import PartitionSpec as P

HEAD_DIM = 128
FEAT = 16
WINDOW = 64


HIGH = lax.Precision.HIGH


def passed_along(block, axis, distance):
    devices = range(lax.axis_size(axis))
    route = [(i - distance, i) for i in devices if i - distance in devices]
    return lax.ppermute(block, axis, route)


def fold_pairs(width):
    upper = [i * width + j for i in range(width) for j in range(i, width)]
    place = {pair: n for n, pair in enumerate(upper)}
    full = [place[min(i, j) * width + max(i, j)] for i in range(width) for j in range(width)]
    keep = np.concatenate([np.arange(1 + width), 1 + width + np.array(upper)])
    back = np.concatenate([np.arange(1 + width), 1 + width + np.array(full)])
    return keep, back


def carried_in(state, normal, last, axis, width):
    place = lax.axis_index(axis)
    length = lax.axis_size(axis)
    keep, back = fold_pairs(width)
    state = jnp.take(state, keep, axis=1)
    normal = jnp.take(normal, keep, axis=1)
    heads, features, lanes = state.shape
    extra = -(-(features + 1) // lanes)
    tag = last.astype(jnp.float32)[0]
    row, column = features + features // lanes, features % lanes

    def packed_of(part, part_normal, part_tag):
        tagged = jnp.concatenate(
            [part_normal, jnp.broadcast_to(part_tag, (heads, 1))], axis=1
        )
        tagged = jnp.pad(tagged, ((0, 0), (0, extra * lanes - features - 1)))
        return jnp.concatenate([part, tagged.reshape(heads, extra, lanes)], axis=1)

    own = packed_of(state, normal, tag)
    before = jnp.zeros_like(own)
    before_tag = jnp.float32(-1.0)
    span, radix = 1, 4
    inclusive = own
    while span < length:
        received = [
            (step * span, passed_along(inclusive, axis, step * span))
            for step in range(1, radix)
            if step * span < length
        ]
        if span == 1:
            before = jnp.where(place >= 1, received[0][1], 0.0)
            before_tag = jnp.where(place >= 1, before[0, row, column], -1.0)
            received = received[1:]
        for distance, early in received:
            absorb = (place >= distance) & (early[0, row, column] == before_tag)
            before = before + jnp.where(absorb, early, 0.0)
        before = before.at[:, row, column].set(before_tag)
        inclusive = own + jnp.where(before_tag == tag, before, 0.0)
        inclusive = inclusive.at[:, row, column].set(tag)
        span *= radix
    flat = before[:, features:].reshape(heads, extra * lanes)
    return (
        jnp.take(before[:, :features], back, axis=1),
        jnp.take(flat[:, :features], back, axis=1),
        before_tag,
    )


def taylor_map(values):
    width = values.shape[-1]
    square = (values[..., :, None] * values[..., None, :]).reshape(
        values.shape[:-1] + (width * width,)
    )
    ones = jnp.ones(values.shape[:-1] + (1,), values.dtype)
    return jnp.concatenate(
        [ones, values * width ** (-0.25), square * (0.5**0.5 / width**0.5)], axis=-1
    )


def heads_split(flat, width):
    return flat.reshape(flat.shape[0], -1, width).transpose(1, 0, 2)


def body(tokens, segment, w_feat_q, w_feat_k, w_query, w_key, w_value, w_out):
    weights = (w_feat_q, w_feat_k, w_query, w_key, w_value)
    piece = lax.all_gather(tokens, "tp", axis=0, tiled=True)
    joined_bf = jnp.concatenate(
        [
            jnp.dot(piece, weight, preferred_element_type=jnp.float32).astype(jnp.bfloat16)
            for weight in weights
        ],
        axis=1,
    )
    joined = lax.optimization_barrier(joined_bf).astype(jnp.float32)
    feat_width = w_feat_q.shape[1]
    head_width = w_query.shape[1]
    offset_w = 2 * feat_width
    feat_q = heads_split(joined[:, :feat_width], FEAT)
    feat_k = heads_split(joined[:, feat_width:offset_w], FEAT)
    value = heads_split(joined[:, offset_w + 2 * head_width :], HEAD_DIM)
    feat_q_bf = heads_split(joined_bf[:, :feat_width], FEAT)
    feat_k_bf = heads_split(joined_bf[:, feat_width:offset_w], FEAT)
    query_bf = heads_split(joined_bf[:, offset_w : offset_w + head_width], HEAD_DIM)
    key_all_bf = heads_split(
        joined_bf[:, offset_w + head_width : offset_w + 2 * head_width], HEAD_DIM
    )
    rows_here = segment.shape[0]
    key_tail_bf = key_all_bf[:, -WINDOW:]
    value_tail_bf = heads_split(joined_bf[-WINDOW:, offset_w + 2 * head_width :], HEAD_DIM)
    seg_mark = (segment[-WINDOW:] + 1).astype(jnp.bfloat16)
    tail_key, tail_value, tail_mark = passed_along((key_tail_bf, value_tail_bf, seg_mark), "ctx", 1)
    mapped_k = taylor_map(feat_k) * (segment == segment[-1])[None, :, None].astype(jnp.float32)
    own_state = jnp.einsum("htf,htd->hfd", mapped_k, value, precision=HIGH)
    own_normal = jnp.sum(mapped_k, axis=1)
    carried_state, carried_normal, carried_last = carried_in(
        own_state, own_normal, segment[-1:], "ctx", FEAT
    )
    seg_float = segment.astype(jnp.float32)
    key_rows = jnp.concatenate([tail_key, key_all_bf], axis=1)
    value_rows = jnp.concatenate([tail_value.astype(jnp.float32), value], axis=1)
    key_seg = jnp.concatenate([tail_mark.astype(jnp.float32), seg_float + 1.0])
    owners = lax.axis_size("tp")
    own = rows_here // owners
    chunks = 2
    sub = own // chunks
    heads = feat_q.shape[0]

    def pick(array, j):
        shape = array.shape
        grouped = array.reshape(shape[:-2] + (owners, own, shape[-1]))
        return grouped[..., sub * j : sub * (j + 1), :].reshape(shape[:-2] + (owners * sub, shape[-1]))

    local = np.arange(sub)
    reach = np.arange(sub + WINDOW)
    near = (reach[None, :] <= local[:, None] + WINDOW) & (reach[None, :] > local[:, None])
    pieces = []
    for j in range(chunks):
        query_pos = (np.arange(owners)[:, None] * own + sub * j + local[None, :]).reshape(-1)
        key_pos = np.arange(rows_here)
        seg_here = seg_float.reshape(owners, own)[:, sub * j : sub * (j + 1)].reshape(-1)
        allowed = (seg_here[:, None] == seg_float[None, :]) & (key_pos[None, :] <= query_pos[:, None])
        inner = (
            jnp.einsum(
                "hsf,htf->hst",
                pick(feat_q_bf, j),
                feat_k_bf,
                preferred_element_type=jnp.float32,
            )
            / FEAT**0.5
        )
        kernel = jnp.where(allowed[None], 1.0 + inner + 0.5 * inner * inner, 0.0)
        numerator = jnp.einsum("hst,htd->hsd", kernel, value, precision=HIGH)
        denominator = jnp.sum(kernel, axis=-1)
        mapped_q = taylor_map(pick(feat_q, j))
        carried = (seg_here == carried_last)[None, :]
        numerator = numerator + jnp.where(
            carried[..., None],
            jnp.einsum("hsf,hfd->hsd", mapped_q, carried_state, precision=HIGH),
            0.0,
        )
        denominator = denominator + jnp.where(
            carried, jnp.einsum("hsf,hf->hs", mapped_q, carried_normal, precision=HIGH), 0.0
        )
        linear_part = numerator / denominator[..., None]
        starts = [b * own + sub * j for b in range(owners)]
        key_blocks = jnp.stack([key_rows[:, s : s + sub + WINDOW] for s in starts], axis=1)
        value_blocks = jnp.stack([value_rows[:, s : s + sub + WINDOW] for s in starts], axis=1)
        seg_blocks = jnp.stack([key_seg[s : s + sub + WINDOW] for s in starts], axis=0)
        query_blocks = pick(query_bf, j).reshape(heads, owners, sub, HEAD_DIM)
        visible = near[None] & (seg_blocks[:, None, :] == seg_here.reshape(owners, sub)[:, :, None] + 1.0)
        scores = (
            jnp.einsum(
                "hbsd,hbtd->hbst",
                query_blocks,
                key_blocks,
                preferred_element_type=jnp.float32,
            )
            / HEAD_DIM**0.5
        )
        scores = jnp.where(visible[None], scores, -jnp.inf)
        peak = jnp.max(scores, axis=-1, keepdims=True)
        expo = jnp.exp(scores - peak)
        window_part = (
            jnp.einsum("hbst,hbtd->hbsd", expo, value_blocks, precision=HIGH)
            / jnp.sum(expo, axis=-1)[..., None]
        ).reshape(heads, owners * sub, HEAD_DIM)
        mixed = (
            (linear_part + window_part)
            .transpose(1, 0, 2)
            .reshape(owners * sub, head_width)
            .astype(jnp.bfloat16)
        )
        pieces.append(
            lax.psum_scatter(
                jnp.dot(mixed, w_out, preferred_element_type=jnp.float32),
                "tp",
                scatter_dimension=0,
                tiled=True,
            ).astype(jnp.bfloat16)
        )
    return jnp.concatenate(pieces, axis=0)


def solution(mesh):
    in_specs = (
        P(("ctx", "tp"), None),
        P("ctx"),
        P(None, "tp"),
        P(None, "tp"),
        P(None, "tp"),
        P(None, "tp"),
        P(None, "tp"),
        P("tp", None),
    )
    out_specs = P(("ctx", "tp"), None)
    return jax.shard_map(body, mesh=mesh, in_specs=in_specs, out_specs=out_specs, check_vma=False)
```

```python
import jax
import numpy as np
import jax.numpy as jnp
from jax import lax
from jax.sharding import PartitionSpec as P

HEAD_DIM = 128
FEAT = 16
WINDOW = 64


HIGH = lax.Precision.HIGH


def passed_along(block, axis, distance):
    devices = range(lax.axis_size(axis))
    route = [(i - distance, i) for i in devices if i - distance in devices]
    return lax.ppermute(block, axis, route)


def fold_pairs(width):
    upper = [i * width + j for i in range(width) for j in range(i, width)]
    place = {pair: n for n, pair in enumerate(upper)}
    full = [place[min(i, j) * width + max(i, j)] for i in range(width) for j in range(width)]
    keep = np.concatenate([np.arange(1 + width), 1 + width + np.array(upper)])
    back = np.concatenate([np.arange(1 + width), 1 + width + np.array(full)])
    return keep, back


def carried_in(state, normal, last, axis, width):
    place = lax.axis_index(axis)
    length = lax.axis_size(axis)
    keep, back = fold_pairs(width)
    state = jnp.take(state, keep, axis=1)
    normal = jnp.take(normal, keep, axis=1)
    heads, features, lanes = state.shape
    extra = -(-(features + 1) // lanes)
    row, column = features + features // lanes, features % lanes
    tagged = jnp.concatenate(
        [normal, jnp.broadcast_to(last.astype(jnp.float32)[0], (heads, 1))], axis=1
    )
    tagged = jnp.pad(tagged, ((0, 0), (0, extra * lanes - features - 1)))
    packed = jnp.concatenate([state, tagged.reshape(heads, extra, lanes)], axis=1)
    everything = lax.all_gather(packed, axis)
    tags = everything[:, 0, row, column]
    order = jnp.arange(length)
    before_tag = jnp.sum(jnp.where(order == place - 1, tags, 0.0))
    before_tag = jnp.where(place >= 1, before_tag, -1.0)
    chosen = (order < place) & (tags == before_tag)
    before = jnp.sum(jnp.where(chosen[:, None, None, None], everything, 0.0), axis=0)
    flat = before[:, features:].reshape(heads, extra * lanes)
    return (
        jnp.take(before[:, :features], back, axis=1),
        jnp.take(flat[:, :features], back, axis=1),
        before_tag,
    )


def taylor_map(values):
    width = values.shape[-1]
    square = (values[..., :, None] * values[..., None, :]).reshape(
        values.shape[:-1] + (width * width,)
    )
    ones = jnp.ones(values.shape[:-1] + (1,), values.dtype)
    return jnp.concatenate(
        [ones, values * width ** (-0.25), square * (0.5**0.5 / width**0.5)], axis=-1
    )


def heads_split(flat, width):
    return flat.reshape(flat.shape[0], -1, width).transpose(1, 0, 2)


def body(tokens, segment, w_feat_q, w_feat_k, w_query, w_key, w_value, w_out):
    weights = (w_feat_q, w_feat_k, w_query, w_key, w_value)
    piece = lax.all_gather(tokens, "tp", axis=0, tiled=True)
    joined_bf = jnp.concatenate(
        [
            jnp.dot(piece, weight, preferred_element_type=jnp.float32).astype(jnp.bfloat16)
            for weight in weights
        ],
        axis=1,
    )
    joined = lax.optimization_barrier(joined_bf).astype(jnp.float32)
    feat_width = w_feat_q.shape[1]
    head_width = w_query.shape[1]
    offset_w = 2 * feat_width
    feat_q = heads_split(joined[:, :feat_width], FEAT)
    feat_k = heads_split(joined[:, feat_width:offset_w], FEAT)
    value = heads_split(joined[:, offset_w + 2 * head_width :], HEAD_DIM)
    feat_q_bf = heads_split(joined_bf[:, :feat_width], FEAT)
    feat_k_bf = heads_split(joined_bf[:, feat_width:offset_w], FEAT)
    query_bf = heads_split(joined_bf[:, offset_w : offset_w + head_width], HEAD_DIM)
    key_all_bf = heads_split(
        joined_bf[:, offset_w + head_width : offset_w + 2 * head_width], HEAD_DIM
    )
    rows_here = segment.shape[0]
    key_tail_bf = key_all_bf[:, -WINDOW:]
    value_tail_bf = heads_split(joined_bf[-WINDOW:, offset_w + 2 * head_width :], HEAD_DIM)
    seg_mark = (segment[-WINDOW:] + 1).astype(jnp.bfloat16)
    tail_key, tail_value, tail_mark = passed_along((key_tail_bf, value_tail_bf, seg_mark), "ctx", 1)
    mapped_k = taylor_map(feat_k) * (segment == segment[-1])[None, :, None].astype(jnp.float32)
    own_state = jnp.einsum("htf,htd->hfd", mapped_k, value, precision=HIGH)
    own_normal = jnp.sum(mapped_k, axis=1)
    carried_state, carried_normal, carried_last = carried_in(
        own_state, own_normal, segment[-1:], "ctx", FEAT
    )
    seg_float = segment.astype(jnp.float32)
    key_rows = jnp.concatenate([tail_key, key_all_bf], axis=1)
    value_rows = jnp.concatenate([tail_value.astype(jnp.float32), value], axis=1)
    key_seg = jnp.concatenate([tail_mark.astype(jnp.float32), seg_float + 1.0])
    owners = lax.axis_size("tp")
    own = rows_here // owners
    chunks = 2
    sub = own // chunks
    heads = feat_q.shape[0]

    def pick(array, j):
        shape = array.shape
        grouped = array.reshape(shape[:-2] + (owners, own, shape[-1]))
        return grouped[..., sub * j : sub * (j + 1), :].reshape(shape[:-2] + (owners * sub, shape[-1]))

    local = np.arange(sub)
    reach = np.arange(sub + WINDOW)
    near = (reach[None, :] <= local[:, None] + WINDOW) & (reach[None, :] > local[:, None])
    pieces = []
    for j in range(chunks):
        query_pos = (np.arange(owners)[:, None] * own + sub * j + local[None, :]).reshape(-1)
        key_pos = np.arange(rows_here)
        seg_here = seg_float.reshape(owners, own)[:, sub * j : sub * (j + 1)].reshape(-1)
        allowed = (seg_here[:, None] == seg_float[None, :]) & (key_pos[None, :] <= query_pos[:, None])
        inner = (
            jnp.einsum(
                "hsf,htf->hst",
                pick(feat_q_bf, j),
                feat_k_bf,
                preferred_element_type=jnp.float32,
            )
            / FEAT**0.5
        )
        kernel = jnp.where(allowed[None], 1.0 + inner + 0.5 * inner * inner, 0.0)
        numerator = jnp.einsum("hst,htd->hsd", kernel, value, precision=HIGH)
        denominator = jnp.sum(kernel, axis=-1)
        mapped_q = taylor_map(pick(feat_q, j))
        carried = (seg_here == carried_last)[None, :]
        numerator = numerator + jnp.where(
            carried[..., None],
            jnp.einsum("hsf,hfd->hsd", mapped_q, carried_state, precision=HIGH),
            0.0,
        )
        denominator = denominator + jnp.where(
            carried, jnp.einsum("hsf,hf->hs", mapped_q, carried_normal, precision=HIGH), 0.0
        )
        linear_part = numerator / denominator[..., None]
        starts = [b * own + sub * j for b in range(owners)]
        key_blocks = jnp.stack([key_rows[:, s : s + sub + WINDOW] for s in starts], axis=1)
        value_blocks = jnp.stack([value_rows[:, s : s + sub + WINDOW] for s in starts], axis=1)
        seg_blocks = jnp.stack([key_seg[s : s + sub + WINDOW] for s in starts], axis=0)
        query_blocks = pick(query_bf, j).reshape(heads, owners, sub, HEAD_DIM)
        visible = near[None] & (seg_blocks[:, None, :] == seg_here.reshape(owners, sub)[:, :, None] + 1.0)
        scores = (
            jnp.einsum(
                "hbsd,hbtd->hbst",
                query_blocks,
                key_blocks,
                preferred_element_type=jnp.float32,
            )
            / HEAD_DIM**0.5
        )
        scores = jnp.where(visible[None], scores, -jnp.inf)
        peak = jnp.max(scores, axis=-1, keepdims=True)
        expo = jnp.exp(scores - peak)
        window_part = (
            jnp.einsum("hbst,hbtd->hbsd", expo, value_blocks, precision=HIGH)
            / jnp.sum(expo, axis=-1)[..., None]
        ).reshape(heads, owners * sub, HEAD_DIM)
        mixed = (
            (linear_part + window_part)
            .transpose(1, 0, 2)
            .reshape(owners * sub, head_width)
            .astype(jnp.bfloat16)
        )
        pieces.append(
            lax.psum_scatter(
                jnp.dot(mixed, w_out, preferred_element_type=jnp.float32),
                "tp",
                scatter_dimension=0,
                tiled=True,
            ).astype(jnp.bfloat16)
        )
    return jnp.concatenate(pieces, axis=0)


def solution(mesh):
    in_specs = (
        P(("ctx", "tp"), None),
        P("ctx"),
        P(None, "tp"),
        P(None, "tp"),
        P(None, "tp"),
        P(None, "tp"),
        P(None, "tp"),
        P("tp", None),
    )
    out_specs = P(("ctx", "tp"), None)
    return jax.shard_map(body, mesh=mesh, in_specs=in_specs, out_specs=out_specs, check_vma=False)
```

```python
import jax
import numpy as np
import jax.numpy as jnp
from jax import lax
from jax.sharding import PartitionSpec as P

HEAD_DIM = 128
FEAT = 16
WINDOW = 64


HIGH = lax.Precision.HIGH


def passed_along(block, axis, distance):
    devices = range(lax.axis_size(axis))
    route = [(i - distance, i) for i in devices if i - distance in devices]
    return lax.ppermute(block, axis, route)


def fold_pairs(width):
    upper = [i * width + j for i in range(width) for j in range(i, width)]
    place = {pair: n for n, pair in enumerate(upper)}
    full = [place[min(i, j) * width + max(i, j)] for i in range(width) for j in range(width)]
    keep = np.concatenate([np.arange(1 + width), 1 + width + np.array(upper)])
    back = np.concatenate([np.arange(1 + width), 1 + width + np.array(full)])
    return keep, back


def carried_in(state, normal, last, axis, width):
    place = lax.axis_index(axis)
    length = lax.axis_size(axis)
    keep, back = fold_pairs(width)
    state = jnp.take(state, keep, axis=1)
    normal = jnp.take(normal, keep, axis=1)
    heads, features, lanes = state.shape
    extra = -(-(features + 1) // lanes)
    row, column = features + features // lanes, features % lanes
    tagged = jnp.concatenate(
        [normal, jnp.broadcast_to(last.astype(jnp.float32)[0], (heads, 1))], axis=1
    )
    tagged = jnp.pad(tagged, ((0, 0), (0, extra * lanes - features - 1)))
    packed = jnp.concatenate([state, tagged.reshape(heads, extra, lanes)], axis=1)
    everything = lax.all_gather(packed, axis)
    tags = everything[:, 0, row, column]
    order = jnp.arange(length)
    before_tag = jnp.sum(jnp.where(order == place - 1, tags, 0.0))
    before_tag = jnp.where(place >= 1, before_tag, -1.0)
    chosen = (order < place) & (tags == before_tag)
    before = jnp.sum(jnp.where(chosen[:, None, None, None], everything, 0.0), axis=0)
    flat = before[:, features:].reshape(heads, extra * lanes)
    return (
        jnp.take(before[:, :features], back, axis=1),
        jnp.take(flat[:, :features], back, axis=1),
        before_tag,
    )


def taylor_map(values):
    width = values.shape[-1]
    square = (values[..., :, None] * values[..., None, :]).reshape(
        values.shape[:-1] + (width * width,)
    )
    ones = jnp.ones(values.shape[:-1] + (1,), values.dtype)
    return jnp.concatenate(
        [ones, values * width ** (-0.25), square * (0.5**0.5 / width**0.5)], axis=-1
    )


def heads_split(flat, width):
    return flat.reshape(flat.shape[0], -1, width).transpose(1, 0, 2)


def body(tokens, segment, w_feat_q, w_feat_k, w_query, w_key, w_value, w_out):
    piece = lax.all_gather(tokens, "tp", axis=0, tiled=True)

    def project(weight, width):
        rounded = jnp.dot(piece, weight, preferred_element_type=jnp.float32).astype(jnp.bfloat16)
        return heads_split(lax.optimization_barrier(rounded), width)

    feat_k_bf = project(w_feat_k, FEAT)
    value_bf = project(w_value, HEAD_DIM)
    feat_q_bf = project(w_feat_q, FEAT)
    query_bf = project(w_query, HEAD_DIM)
    key_all_bf = project(w_key, HEAD_DIM)
    feat_q = feat_q_bf.astype(jnp.float32)
    feat_k = feat_k_bf.astype(jnp.float32)
    value = value_bf.astype(jnp.float32)
    head_width = w_query.shape[1]
    rows_here = segment.shape[0]
    key_tail_bf = key_all_bf[:, -WINDOW:]
    value_tail_bf = value_bf[:, -WINDOW:]
    seg_mark = (segment[-WINDOW:] + 1).astype(jnp.bfloat16)
    tail_key, tail_value, tail_mark = passed_along((key_tail_bf, value_tail_bf, seg_mark), "ctx", 1)
    mapped_k = taylor_map(feat_k) * (segment == segment[-1])[None, :, None].astype(jnp.float32)
    own_state = jnp.einsum("htf,htd->hfd", mapped_k, value, precision=HIGH)
    own_normal = jnp.sum(mapped_k, axis=1)
    carried_state, carried_normal, carried_last = carried_in(
        own_state, own_normal, segment[-1:], "ctx", FEAT
    )
    seg_float = segment.astype(jnp.float32)
    key_rows = jnp.concatenate([tail_key, key_all_bf], axis=1)
    value_rows = jnp.concatenate([tail_value.astype(jnp.float32), value], axis=1)
    key_seg = jnp.concatenate([tail_mark.astype(jnp.float32), seg_float + 1.0])
    owners = lax.axis_size("tp")
    own = rows_here // owners
    chunks = 4
    sub = own // chunks
    heads = feat_q.shape[0]

    def pick(array, j):
        shape = array.shape
        grouped = array.reshape(shape[:-2] + (owners, own, shape[-1]))
        return grouped[..., sub * j : sub * (j + 1), :].reshape(shape[:-2] + (owners * sub, shape[-1]))

    local = np.arange(sub)
    reach = np.arange(sub + WINDOW)
    near = (reach[None, :] <= local[:, None] + WINDOW) & (reach[None, :] > local[:, None])
    pieces = []
    for j in range(chunks):
        query_pos = (np.arange(owners)[:, None] * own + sub * j + local[None, :]).reshape(-1)
        key_pos = np.arange(rows_here)
        seg_here = seg_float.reshape(owners, own)[:, sub * j : sub * (j + 1)].reshape(-1)
        allowed = (seg_here[:, None] == seg_float[None, :]) & (key_pos[None, :] <= query_pos[:, None])
        inner = (
            jnp.einsum(
                "hsf,htf->hst",
                pick(feat_q_bf, j),
                feat_k_bf,
                preferred_element_type=jnp.float32,
            )
            / FEAT**0.5
        )
        kernel = jnp.where(allowed[None], 1.0 + inner + 0.5 * inner * inner, 0.0)
        numerator = jnp.einsum("hst,htd->hsd", kernel, value, precision=HIGH)
        denominator = jnp.sum(kernel, axis=-1)
        mapped_q = taylor_map(pick(feat_q, j))
        carried = (seg_here == carried_last)[None, :]
        numerator = numerator + jnp.where(
            carried[..., None],
            jnp.einsum("hsf,hfd->hsd", mapped_q, carried_state, precision=HIGH),
            0.0,
        )
        denominator = denominator + jnp.where(
            carried, jnp.einsum("hsf,hf->hs", mapped_q, carried_normal, precision=HIGH), 0.0
        )
        linear_part = numerator / denominator[..., None]
        starts = [b * own + sub * j for b in range(owners)]
        key_blocks = jnp.stack([key_rows[:, s : s + sub + WINDOW] for s in starts], axis=1)
        value_blocks = jnp.stack([value_rows[:, s : s + sub + WINDOW] for s in starts], axis=1)
        seg_blocks = jnp.stack([key_seg[s : s + sub + WINDOW] for s in starts], axis=0)
        query_blocks = pick(query_bf, j).reshape(heads, owners, sub, HEAD_DIM)
        visible = near[None] & (seg_blocks[:, None, :] == seg_here.reshape(owners, sub)[:, :, None] + 1.0)
        scores = (
            jnp.einsum(
                "hbsd,hbtd->hbst",
                query_blocks,
                key_blocks,
                preferred_element_type=jnp.float32,
            )
            / HEAD_DIM**0.5
        )
        scores = jnp.where(visible[None], scores, -jnp.inf)
        peak = jnp.max(scores, axis=-1, keepdims=True)
        expo = jnp.exp(scores - peak)
        window_part = (
            jnp.einsum("hbst,hbtd->hbsd", expo, value_blocks, precision=HIGH)
            / jnp.sum(expo, axis=-1)[..., None]
        ).reshape(heads, owners * sub, HEAD_DIM)
        mixed = (
            (linear_part + window_part)
            .transpose(1, 0, 2)
            .reshape(owners * sub, head_width)
            .astype(jnp.bfloat16)
        )
        pieces.append(
            lax.psum_scatter(
                jnp.dot(mixed, w_out, preferred_element_type=jnp.float32),
                "tp",
                scatter_dimension=0,
                tiled=True,
            ).astype(jnp.bfloat16)
        )
    return jnp.concatenate(pieces, axis=0)


def solution(mesh):
    in_specs = (
        P(("ctx", "tp"), None),
        P("ctx"),
        P(None, "tp"),
        P(None, "tp"),
        P(None, "tp"),
        P(None, "tp"),
        P(None, "tp"),
        P("tp", None),
    )
    out_specs = P(("ctx", "tp"), None)
    return jax.shard_map(body, mesh=mesh, in_specs=in_specs, out_specs=out_specs, check_vma=False)
```

```python
import jax
import numpy as np
import jax.numpy as jnp
from jax import lax
from jax.sharding import PartitionSpec as P

HEAD_DIM = 128
FEAT = 16
WINDOW = 64


HIGH = lax.Precision.HIGH


def passed_along(block, axis, distance):
    devices = range(lax.axis_size(axis))
    route = [(i - distance, i) for i in devices if i - distance in devices]
    return lax.ppermute(block, axis, route)


def fold_pairs(width):
    upper = [i * width + j for i in range(width) for j in range(i, width)]
    place = {pair: n for n, pair in enumerate(upper)}
    full = [place[min(i, j) * width + max(i, j)] for i in range(width) for j in range(width)]
    keep = np.concatenate([np.arange(1 + width), 1 + width + np.array(upper)])
    back = np.concatenate([np.arange(1 + width), 1 + width + np.array(full)])
    return keep, back


def carried_in(state, normal, last, axis, width):
    place = lax.axis_index(axis)
    length = lax.axis_size(axis)
    keep, back = fold_pairs(width)
    state = jnp.take(state, keep, axis=1)
    normal = jnp.take(normal, keep, axis=1)
    heads, features, lanes = state.shape
    extra = -(-(features + 1) // lanes)
    row, column = features + features // lanes, features % lanes
    tagged = jnp.concatenate(
        [normal, jnp.broadcast_to(last.astype(jnp.float32)[0], (heads, 1))], axis=1
    )
    tagged = jnp.pad(tagged, ((0, 0), (0, extra * lanes - features - 1)))
    packed = jnp.concatenate([state, tagged.reshape(heads, extra, lanes)], axis=1)
    everything = lax.all_gather(packed, axis)
    tags = everything[:, 0, row, column]
    order = jnp.arange(length)
    before_tag = jnp.sum(jnp.where(order == place - 1, tags, 0.0))
    before_tag = jnp.where(place >= 1, before_tag, -1.0)
    chosen = (order < place) & (tags == before_tag)
    before = jnp.sum(jnp.where(chosen[:, None, None, None], everything, 0.0), axis=0)
    flat = before[:, features:].reshape(heads, extra * lanes)
    return (
        jnp.take(before[:, :features], back, axis=1),
        jnp.take(flat[:, :features], back, axis=1),
        before_tag,
    )


def taylor_map(values):
    width = values.shape[-1]
    square = (values[..., :, None] * values[..., None, :]).reshape(
        values.shape[:-1] + (width * width,)
    )
    ones = jnp.ones(values.shape[:-1] + (1,), values.dtype)
    return jnp.concatenate(
        [ones, values * width ** (-0.25), square * (0.5**0.5 / width**0.5)], axis=-1
    )


def heads_split(flat, width):
    return flat.reshape(flat.shape[0], -1, width).transpose(1, 0, 2)


def body(tokens, segment, w_feat_q, w_feat_k, w_query, w_key, w_value, w_out):
    piece = lax.all_gather(tokens, "tp", axis=0, tiled=True)

    def project(weight, width):
        rounded = jnp.dot(piece, weight, preferred_element_type=jnp.float32).astype(jnp.bfloat16)
        return heads_split(lax.optimization_barrier(rounded), width)

    feat_k_bf = project(w_feat_k, FEAT)
    value_bf = project(w_value, HEAD_DIM)
    feat_q_bf = project(w_feat_q, FEAT)
    query_bf = project(w_query, HEAD_DIM)
    key_all_bf = project(w_key, HEAD_DIM)
    feat_q = feat_q_bf.astype(jnp.float32)
    feat_k = feat_k_bf.astype(jnp.float32)
    value = value_bf.astype(jnp.float32)
    head_width = w_query.shape[1]
    rows_here = segment.shape[0]
    key_tail_bf = key_all_bf[:, -WINDOW:]
    value_tail_bf = value_bf[:, -WINDOW:]
    seg_mark = (segment[-WINDOW:] + 1).astype(jnp.bfloat16)
    tail_key, tail_value, tail_mark = passed_along((key_tail_bf, value_tail_bf, seg_mark), "ctx", 1)
    mapped_k = taylor_map(feat_k) * (segment == segment[-1])[None, :, None].astype(jnp.float32)
    own_state = jnp.einsum("htf,htd->hfd", mapped_k, value, precision=HIGH)
    own_normal = jnp.sum(mapped_k, axis=1)
    carried_state, carried_normal, carried_last = carried_in(
        own_state, own_normal, segment[-1:], "ctx", FEAT
    )
    seg_float = segment.astype(jnp.float32)
    key_rows = jnp.concatenate([tail_key, key_all_bf], axis=1)
    value_rows = jnp.concatenate([tail_value.astype(jnp.float32), value], axis=1)
    key_seg = jnp.concatenate([tail_mark.astype(jnp.float32), seg_float + 1.0])
    owners = lax.axis_size("tp")
    own = rows_here // owners
    chunks = 2
    sub = own // chunks
    heads = feat_q.shape[0]

    def pick(array, j):
        shape = array.shape
        grouped = array.reshape(shape[:-2] + (owners, own, shape[-1]))
        return grouped[..., sub * j : sub * (j + 1), :].reshape(shape[:-2] + (owners * sub, shape[-1]))

    local = np.arange(sub)
    reach = np.arange(sub + WINDOW)
    near = (reach[None, :] <= local[:, None] + WINDOW) & (reach[None, :] > local[:, None])
    pieces = []
    for j in range(chunks):
        query_pos = (np.arange(owners)[:, None] * own + sub * j + local[None, :]).reshape(-1)
        key_pos = np.arange(rows_here)
        seg_here = seg_float.reshape(owners, own)[:, sub * j : sub * (j + 1)].reshape(-1)
        allowed = (seg_here[:, None] == seg_float[None, :]) & (key_pos[None, :] <= query_pos[:, None])
        inner = (
            jnp.einsum(
                "hsf,htf->hst",
                pick(feat_q_bf, j),
                feat_k_bf,
                preferred_element_type=jnp.float32,
            )
            / FEAT**0.5
        )
        kernel = jnp.where(allowed[None], 1.0 + inner + 0.5 * inner * inner, 0.0)
        numerator = jnp.einsum("hst,htd->hsd", kernel, value, precision=HIGH)
        denominator = jnp.sum(kernel, axis=-1)
        mapped_q = taylor_map(pick(feat_q, j))
        carried = (seg_here == carried_last)[None, :]
        numerator = numerator + jnp.where(
            carried[..., None],
            jnp.einsum("hsf,hfd->hsd", mapped_q, carried_state, precision=HIGH),
            0.0,
        )
        denominator = denominator + jnp.where(
            carried, jnp.einsum("hsf,hf->hs", mapped_q, carried_normal, precision=HIGH), 0.0
        )
        linear_part = numerator / denominator[..., None]
        starts = [b * own + sub * j for b in range(owners)]
        key_blocks = jnp.stack([key_rows[:, s : s + sub + WINDOW] for s in starts], axis=1)
        value_blocks = jnp.stack([value_rows[:, s : s + sub + WINDOW] for s in starts], axis=1)
        seg_blocks = jnp.stack([key_seg[s : s + sub + WINDOW] for s in starts], axis=0)
        query_blocks = pick(query_bf, j).reshape(heads, owners, sub, HEAD_DIM)
        visible = near[None] & (seg_blocks[:, None, :] == seg_here.reshape(owners, sub)[:, :, None] + 1.0)
        scores = (
            jnp.einsum(
                "hbsd,hbtd->hbst",
                query_blocks,
                key_blocks,
                preferred_element_type=jnp.float32,
            )
            / HEAD_DIM**0.5
        )
        scores = jnp.where(visible[None], scores, -jnp.inf)
        peak = jnp.max(scores, axis=-1, keepdims=True)
        expo = jnp.exp(scores - peak)
        window_part = (
            jnp.einsum("hbst,hbtd->hbsd", expo, value_blocks, precision=HIGH)
            / jnp.sum(expo, axis=-1)[..., None]
        ).reshape(heads, owners * sub, HEAD_DIM)
        mixed = (
            (linear_part + window_part)
            .transpose(1, 0, 2)
            .reshape(owners * sub, head_width)
            .astype(jnp.bfloat16)
        )
        pieces.append(
            lax.psum_scatter(
                jnp.dot(mixed, w_out, preferred_element_type=jnp.float32),
                "tp",
                scatter_dimension=0,
                tiled=True,
            ).astype(jnp.bfloat16)
        )
    return jnp.concatenate(pieces, axis=0)


def solution(mesh):
    in_specs = (
        P(("ctx", "tp"), None),
        P("ctx"),
        P(None, "tp"),
        P(None, "tp"),
        P(None, "tp"),
        P(None, "tp"),
        P(None, "tp"),
        P("tp", None),
    )
    out_specs = P(("ctx", "tp"), None)
    return jax.shard_map(body, mesh=mesh, in_specs=in_specs, out_specs=out_specs, check_vma=False)
```

```python
import jax
import numpy as np
import jax.numpy as jnp
from jax import lax
from jax.sharding import PartitionSpec as P

HEAD_DIM = 128
FEAT = 16
WINDOW = 64


HIGH = lax.Precision.HIGH


def passed_along(block, axis, distance):
    devices = range(lax.axis_size(axis))
    route = [(i - distance, i) for i in devices if i - distance in devices]
    return lax.ppermute(block, axis, route)


def fold_pairs(width):
    upper = [i * width + j for i in range(width) for j in range(i, width)]
    place = {pair: n for n, pair in enumerate(upper)}
    full = [place[min(i, j) * width + max(i, j)] for i in range(width) for j in range(width)]
    keep = np.concatenate([np.arange(1 + width), 1 + width + np.array(upper)])
    back = np.concatenate([np.arange(1 + width), 1 + width + np.array(full)])
    return keep, back


def carried_in(state, normal, last, axis, width):
    place = lax.axis_index(axis)
    length = lax.axis_size(axis)
    keep, back = fold_pairs(width)
    state = jnp.take(state, keep, axis=1)
    normal = jnp.take(normal, keep, axis=1)
    heads, features, lanes = state.shape
    extra = -(-(features + 1) // lanes)
    row, column = features + features // lanes, features % lanes
    tagged = jnp.concatenate(
        [normal, jnp.broadcast_to(last.astype(jnp.float32)[0], (heads, 1))], axis=1
    )
    tagged = jnp.pad(tagged, ((0, 0), (0, extra * lanes - features - 1)))
    packed = jnp.concatenate([state, tagged.reshape(heads, extra, lanes)], axis=1)
    everything = lax.all_gather(packed, axis)
    tags = everything[:, 0, row, column]
    order = jnp.arange(length)
    before_tag = jnp.sum(jnp.where(order == place - 1, tags, 0.0))
    before_tag = jnp.where(place >= 1, before_tag, -1.0)
    chosen = (order < place) & (tags == before_tag)
    before = jnp.sum(jnp.where(chosen[:, None, None, None], everything, 0.0), axis=0)
    flat = before[:, features:].reshape(heads, extra * lanes)
    return (
        jnp.take(before[:, :features], back, axis=1),
        jnp.take(flat[:, :features], back, axis=1),
        before_tag,
    )


def taylor_map(values):
    width = values.shape[-1]
    square = (values[..., :, None] * values[..., None, :]).reshape(
        values.shape[:-1] + (width * width,)
    )
    ones = jnp.ones(values.shape[:-1] + (1,), values.dtype)
    return jnp.concatenate(
        [ones, values * width ** (-0.25), square * (0.5**0.5 / width**0.5)], axis=-1
    )


def heads_split(flat, width):
    return flat.reshape(flat.shape[0], -1, width).transpose(1, 0, 2)


def body(tokens, segment, w_feat_q, w_feat_k, w_query, w_key, w_value, w_out):
    piece = lax.all_gather(tokens, "tp", axis=0, tiled=True)

    def project(weights, widths):
        joined = jnp.concatenate(weights, axis=1)
        rounded = jnp.dot(piece, joined, preferred_element_type=jnp.float32).astype(jnp.bfloat16)
        rounded = lax.optimization_barrier(rounded)
        bounds = np.cumsum([0] + [weight.shape[1] for weight in weights])
        return [
            heads_split(rounded[:, bounds[n] : bounds[n + 1]], width)
            for n, width in enumerate(widths)
        ]

    feat_k_bf, value_bf = project((w_feat_k, w_value), (FEAT, HEAD_DIM))
    feat_q_bf, query_bf, key_all_bf = project((w_feat_q, w_query, w_key), (FEAT, HEAD_DIM, HEAD_DIM))
    feat_q = feat_q_bf.astype(jnp.float32)
    feat_k = feat_k_bf.astype(jnp.float32)
    value = value_bf.astype(jnp.float32)
    head_width = w_query.shape[1]
    rows_here = segment.shape[0]
    key_tail_bf = key_all_bf[:, -WINDOW:]
    value_tail_bf = value_bf[:, -WINDOW:]
    seg_mark = jnp.broadcast_to(
        (segment[-WINDOW:] + 1).astype(jnp.bfloat16)[None, :, None], (key_tail_bf.shape[0], WINDOW, HEAD_DIM)
    )
    tails = passed_along(jnp.concatenate([key_tail_bf, value_tail_bf, seg_mark[:1]], axis=0), "ctx", 1)
    heads_n = key_tail_bf.shape[0]
    tail_key, tail_value = tails[:heads_n], tails[heads_n : 2 * heads_n]
    tail_mark = tails[2 * heads_n, :, 0]
    mapped_k = taylor_map(feat_k) * (segment == segment[-1])[None, :, None].astype(jnp.float32)
    own_state = jnp.einsum("htf,htd->hfd", mapped_k, value, precision=HIGH)
    own_normal = jnp.sum(mapped_k, axis=1)
    carried_state, carried_normal, carried_last = carried_in(
        own_state, own_normal, segment[-1:], "ctx", FEAT
    )
    seg_float = segment.astype(jnp.float32)
    key_rows = jnp.concatenate([tail_key, key_all_bf], axis=1)
    value_rows = jnp.concatenate([tail_value.astype(jnp.float32), value], axis=1)
    key_seg = jnp.concatenate([tail_mark.astype(jnp.float32), seg_float + 1.0])
    owners = lax.axis_size("tp")
    own = rows_here // owners
    chunks = 2
    sub = own // chunks
    heads = feat_q.shape[0]

    def pick(array, j):
        shape = array.shape
        grouped = array.reshape(shape[:-2] + (owners, own, shape[-1]))
        return grouped[..., sub * j : sub * (j + 1), :].reshape(shape[:-2] + (owners * sub, shape[-1]))

    local = np.arange(sub)
    reach = np.arange(sub + WINDOW)
    near = (reach[None, :] <= local[:, None] + WINDOW) & (reach[None, :] > local[:, None])
    pieces = []
    for j in range(chunks):
        query_pos = (np.arange(owners)[:, None] * own + sub * j + local[None, :]).reshape(-1)
        key_pos = np.arange(rows_here)
        seg_here = seg_float.reshape(owners, own)[:, sub * j : sub * (j + 1)].reshape(-1)
        allowed = (seg_here[:, None] == seg_float[None, :]) & (key_pos[None, :] <= query_pos[:, None])
        inner = (
            jnp.einsum(
                "hsf,htf->hst",
                pick(feat_q_bf, j),
                feat_k_bf,
                preferred_element_type=jnp.float32,
            )
            / FEAT**0.5
        )
        kernel = jnp.where(allowed[None], 1.0 + inner + 0.5 * inner * inner, 0.0)
        numerator = jnp.einsum("hst,htd->hsd", kernel, value, precision=HIGH)
        denominator = jnp.sum(kernel, axis=-1)
        mapped_q = taylor_map(pick(feat_q, j))
        carried = (seg_here == carried_last)[None, :]
        numerator = numerator + jnp.where(
            carried[..., None],
            jnp.einsum("hsf,hfd->hsd", mapped_q, carried_state, precision=HIGH),
            0.0,
        )
        denominator = denominator + jnp.where(
            carried, jnp.einsum("hsf,hf->hs", mapped_q, carried_normal, precision=HIGH), 0.0
        )
        linear_part = numerator / denominator[..., None]
        starts = [b * own + sub * j for b in range(owners)]
        key_blocks = jnp.stack([key_rows[:, s : s + sub + WINDOW] for s in starts], axis=1)
        value_blocks = jnp.stack([value_rows[:, s : s + sub + WINDOW] for s in starts], axis=1)
        seg_blocks = jnp.stack([key_seg[s : s + sub + WINDOW] for s in starts], axis=0)
        query_blocks = pick(query_bf, j).reshape(heads, owners, sub, HEAD_DIM)
        visible = near[None] & (seg_blocks[:, None, :] == seg_here.reshape(owners, sub)[:, :, None] + 1.0)
        scores = (
            jnp.einsum(
                "hbsd,hbtd->hbst",
                query_blocks,
                key_blocks,
                preferred_element_type=jnp.float32,
            )
            / HEAD_DIM**0.5
        )
        scores = jnp.where(visible[None], scores, -jnp.inf)
        peak = jnp.max(scores, axis=-1, keepdims=True)
        expo = jnp.exp(scores - peak)
        window_part = (
            jnp.einsum("hbst,hbtd->hbsd", expo, value_blocks, precision=HIGH)
            / jnp.sum(expo, axis=-1)[..., None]
        ).reshape(heads, owners * sub, HEAD_DIM)
        mixed = (
            (linear_part + window_part)
            .transpose(1, 0, 2)
            .reshape(owners * sub, head_width)
            .astype(jnp.bfloat16)
        )
        pieces.append(
            lax.psum_scatter(
                jnp.dot(mixed, w_out, preferred_element_type=jnp.float32),
                "tp",
                scatter_dimension=0,
                tiled=True,
            ).astype(jnp.bfloat16)
        )
    return jnp.concatenate(pieces, axis=0)


def solution(mesh):
    in_specs = (
        P(("ctx", "tp"), None),
        P("ctx"),
        P(None, "tp"),
        P(None, "tp"),
        P(None, "tp"),
        P(None, "tp"),
        P(None, "tp"),
        P("tp", None),
    )
    out_specs = P(("ctx", "tp"), None)
    return jax.shard_map(body, mesh=mesh, in_specs=in_specs, out_specs=out_specs, check_vma=False)
```

```python
import jax
import numpy as np
import jax.numpy as jnp
from jax import lax
from jax.sharding import PartitionSpec as P

HEAD_DIM = 128
FEAT = 16
WINDOW = 64


HIGH = lax.Precision.HIGH


def passed_along(block, axis, distance):
    devices = range(lax.axis_size(axis))
    route = [(i - distance, i) for i in devices if i - distance in devices]
    return lax.ppermute(block, axis, route)


def fold_pairs(width):
    upper = [i * width + j for i in range(width) for j in range(i, width)]
    place = {pair: n for n, pair in enumerate(upper)}
    full = [place[min(i, j) * width + max(i, j)] for i in range(width) for j in range(width)]
    keep = np.concatenate([np.arange(1 + width), 1 + width + np.array(upper)])
    back = np.concatenate([np.arange(1 + width), 1 + width + np.array(full)])
    return keep, back


def carried_in(state, normal, last, axis, width):
    place = lax.axis_index(axis)
    length = lax.axis_size(axis)
    keep, back = fold_pairs(width)
    state = jnp.take(state, keep, axis=1)
    normal = jnp.take(normal, keep, axis=1)
    heads, features, lanes = state.shape
    extra = -(-(features + 1) // lanes)
    row, column = features + features // lanes, features % lanes
    tagged = jnp.concatenate(
        [normal, jnp.broadcast_to(last.astype(jnp.float32)[0], (heads, 1))], axis=1
    )
    tagged = jnp.pad(tagged, ((0, 0), (0, extra * lanes - features - 1)))
    packed = jnp.concatenate([state, tagged.reshape(heads, extra, lanes)], axis=1)
    everything = lax.all_gather(packed, axis)
    tags = everything[:, 0, row, column]
    order = jnp.arange(length)
    before_tag = jnp.sum(jnp.where(order == place - 1, tags, 0.0))
    before_tag = jnp.where(place >= 1, before_tag, -1.0)
    chosen = (order < place) & (tags == before_tag)
    before = jnp.sum(jnp.where(chosen[:, None, None, None], everything, 0.0), axis=0)
    flat = before[:, features:].reshape(heads, extra * lanes)
    return (
        jnp.take(before[:, :features], back, axis=1),
        jnp.take(flat[:, :features], back, axis=1),
        before_tag,
    )


def taylor_map(values):
    width = values.shape[-1]
    square = (values[..., :, None] * values[..., None, :]).reshape(
        values.shape[:-1] + (width * width,)
    )
    ones = jnp.ones(values.shape[:-1] + (1,), values.dtype)
    return jnp.concatenate(
        [ones, values * width ** (-0.25), square * (0.5**0.5 / width**0.5)], axis=-1
    )


def heads_split(flat, width):
    return flat.reshape(flat.shape[0], -1, width).transpose(1, 0, 2)


def body(tokens, segment, w_feat_q, w_feat_k, w_query, w_key, w_value, w_out):
    piece = lax.all_gather(tokens, "tp", axis=0, tiled=True)

    def project(weights, widths):
        joined = jnp.concatenate(weights, axis=1)
        rounded = jnp.dot(piece, joined, preferred_element_type=jnp.float32).astype(jnp.bfloat16)
        rounded = lax.optimization_barrier(rounded)
        bounds = np.cumsum([0] + [weight.shape[1] for weight in weights])
        return [
            heads_split(rounded[:, bounds[n] : bounds[n + 1]], width)
            for n, width in enumerate(widths)
        ]

    feat_k_bf, value_bf = project((w_feat_k, w_value), (FEAT, HEAD_DIM))
    feat_q_bf, query_bf, key_all_bf = project((w_feat_q, w_query, w_key), (FEAT, HEAD_DIM, HEAD_DIM))
    feat_q = feat_q_bf.astype(jnp.float32)
    feat_k = feat_k_bf.astype(jnp.float32)
    value = value_bf.astype(jnp.float32)
    head_width = w_query.shape[1]
    rows_here = segment.shape[0]
    key_tail_bf = key_all_bf[:, -WINDOW:]
    value_tail_bf = value_bf[:, -WINDOW:]
    seg_mark = jnp.broadcast_to(
        (segment[-WINDOW:] + 1).astype(jnp.bfloat16)[None, :, None], (key_tail_bf.shape[0], WINDOW, HEAD_DIM)
    )
    tails = passed_along(jnp.concatenate([key_tail_bf, value_tail_bf, seg_mark[:1]], axis=0), "ctx", 1)
    heads_n = key_tail_bf.shape[0]
    tail_key, tail_value = tails[:heads_n], tails[heads_n : 2 * heads_n]
    tail_mark = tails[2 * heads_n, :, 0]
    mapped_k = taylor_map(feat_k) * (segment == segment[-1])[None, :, None].astype(jnp.float32)
    own_state = jnp.einsum("htf,htd->hfd", mapped_k, value, precision=HIGH)
    own_normal = jnp.sum(mapped_k, axis=1)
    carried_state, carried_normal, carried_last = carried_in(
        own_state, own_normal, segment[-1:], "ctx", FEAT
    )
    seg_float = segment.astype(jnp.float32)
    key_rows = jnp.concatenate([tail_key, key_all_bf], axis=1)
    value_rows = jnp.concatenate([tail_value.astype(jnp.float32), value], axis=1)
    key_seg = jnp.concatenate([tail_mark.astype(jnp.float32), seg_float + 1.0])
    owners = lax.axis_size("tp")
    own = rows_here // owners
    bounds = (0, own // 4, own)
    heads = feat_q.shape[0]

    def pick(array, j):
        shape = array.shape
        grouped = array.reshape(shape[:-2] + (owners, own, shape[-1]))
        taken = grouped[..., bounds[j] : bounds[j + 1], :]
        return taken.reshape(shape[:-2] + (owners * (bounds[j + 1] - bounds[j]), shape[-1]))

    pieces = []
    for j in range(len(bounds) - 1):
        sub = bounds[j + 1] - bounds[j]
        local = np.arange(sub)
        reach = np.arange(sub + WINDOW)
        near = (reach[None, :] <= local[:, None] + WINDOW) & (reach[None, :] > local[:, None])
        query_pos = (np.arange(owners)[:, None] * own + bounds[j] + local[None, :]).reshape(-1)
        key_pos = np.arange(rows_here)
        seg_here = seg_float.reshape(owners, own)[:, bounds[j] : bounds[j + 1]].reshape(-1)
        allowed = (seg_here[:, None] == seg_float[None, :]) & (key_pos[None, :] <= query_pos[:, None])
        inner = (
            jnp.einsum(
                "hsf,htf->hst",
                pick(feat_q_bf, j),
                feat_k_bf,
                preferred_element_type=jnp.float32,
            )
            / FEAT**0.5
        )
        kernel = jnp.where(allowed[None], 1.0 + inner + 0.5 * inner * inner, 0.0)
        numerator = jnp.einsum("hst,htd->hsd", kernel, value, precision=HIGH)
        denominator = jnp.sum(kernel, axis=-1)
        mapped_q = taylor_map(pick(feat_q, j))
        carried = (seg_here == carried_last)[None, :]
        numerator = numerator + jnp.where(
            carried[..., None],
            jnp.einsum("hsf,hfd->hsd", mapped_q, carried_state, precision=HIGH),
            0.0,
        )
        denominator = denominator + jnp.where(
            carried, jnp.einsum("hsf,hf->hs", mapped_q, carried_normal, precision=HIGH), 0.0
        )
        linear_part = numerator / denominator[..., None]
        starts = [b * own + bounds[j] for b in range(owners)]
        key_blocks = jnp.stack([key_rows[:, s : s + sub + WINDOW] for s in starts], axis=1)
        value_blocks = jnp.stack([value_rows[:, s : s + sub + WINDOW] for s in starts], axis=1)
        seg_blocks = jnp.stack([key_seg[s : s + sub + WINDOW] for s in starts], axis=0)
        query_blocks = pick(query_bf, j).reshape(heads, owners, sub, HEAD_DIM)
        visible = near[None] & (seg_blocks[:, None, :] == seg_here.reshape(owners, sub)[:, :, None] + 1.0)
        scores = (
            jnp.einsum(
                "hbsd,hbtd->hbst",
                query_blocks,
                key_blocks,
                preferred_element_type=jnp.float32,
            )
            / HEAD_DIM**0.5
        )
        scores = jnp.where(visible[None], scores, -jnp.inf)
        peak = jnp.max(scores, axis=-1, keepdims=True)
        expo = jnp.exp(scores - peak)
        window_part = (
            jnp.einsum("hbst,hbtd->hbsd", expo, value_blocks, precision=HIGH)
            / jnp.sum(expo, axis=-1)[..., None]
        ).reshape(heads, owners * sub, HEAD_DIM)
        mixed = (
            (linear_part + window_part)
            .transpose(1, 0, 2)
            .reshape(owners * sub, head_width)
            .astype(jnp.bfloat16)
        )
        pieces.append(
            lax.psum_scatter(
                jnp.dot(mixed, w_out, preferred_element_type=jnp.float32),
                "tp",
                scatter_dimension=0,
                tiled=True,
            ).astype(jnp.bfloat16)
        )
    return jnp.concatenate(pieces, axis=0)


def solution(mesh):
    in_specs = (
        P(("ctx", "tp"), None),
        P("ctx"),
        P(None, "tp"),
        P(None, "tp"),
        P(None, "tp"),
        P(None, "tp"),
        P(None, "tp"),
        P("tp", None),
    )
    out_specs = P(("ctx", "tp"), None)
    return jax.shard_map(body, mesh=mesh, in_specs=in_specs, out_specs=out_specs, check_vma=False)
```

```python
import jax
import numpy as np
import jax.numpy as jnp
from jax import lax
from jax.sharding import PartitionSpec as P

HEAD_DIM = 128
FEAT = 16
WINDOW = 64


HIGH = lax.Precision.HIGH


def passed_along(block, axis, distance):
    devices = range(lax.axis_size(axis))
    route = [(i - distance, i) for i in devices if i - distance in devices]
    return lax.ppermute(block, axis, route)


def fold_pairs(width):
    upper = [i * width + j for i in range(width) for j in range(i, width)]
    place = {pair: n for n, pair in enumerate(upper)}
    full = [place[min(i, j) * width + max(i, j)] for i in range(width) for j in range(width)]
    keep = np.concatenate([np.arange(1 + width), 1 + width + np.array(upper)])
    back = np.concatenate([np.arange(1 + width), 1 + width + np.array(full)])
    return keep, back


def carried_in(state, normal, last, axis, width):
    place = lax.axis_index(axis)
    length = lax.axis_size(axis)
    keep, back = fold_pairs(width)
    state = jnp.take(state, keep, axis=1)
    normal = jnp.take(normal, keep, axis=1)
    heads, features, lanes = state.shape
    extra = -(-(features + 1) // lanes)
    row, column = features + features // lanes, features % lanes
    tagged = jnp.concatenate(
        [normal, jnp.broadcast_to(last.astype(jnp.float32)[0], (heads, 1))], axis=1
    )
    tagged = jnp.pad(tagged, ((0, 0), (0, extra * lanes - features - 1)))
    packed = jnp.concatenate([state, tagged.reshape(heads, extra, lanes)], axis=1)
    everything = lax.all_gather(packed, axis)
    tags = everything[:, 0, row, column]
    order = jnp.arange(length)
    before_tag = jnp.sum(jnp.where(order == place - 1, tags, 0.0))
    before_tag = jnp.where(place >= 1, before_tag, -1.0)
    chosen = (order < place) & (tags == before_tag)
    before = jnp.sum(jnp.where(chosen[:, None, None, None], everything, 0.0), axis=0)
    flat = before[:, features:].reshape(heads, extra * lanes)
    return before[:, :features], flat[:, :features], before_tag


def taylor_map(values):
    width = values.shape[-1]
    square = (values[..., :, None] * values[..., None, :]).reshape(
        values.shape[:-1] + (width * width,)
    )
    ones = jnp.ones(values.shape[:-1] + (1,), values.dtype)
    return jnp.concatenate(
        [ones, values * width ** (-0.25), square * (0.5**0.5 / width**0.5)], axis=-1
    )


def heads_split(flat, width):
    return flat.reshape(flat.shape[0], -1, width).transpose(1, 0, 2)


def body(tokens, segment, w_feat_q, w_feat_k, w_query, w_key, w_value, w_out):
    piece = lax.all_gather(tokens, "tp", axis=0, tiled=True)

    def project(weights, widths):
        joined = jnp.concatenate(weights, axis=1)
        rounded = jnp.dot(piece, joined, preferred_element_type=jnp.float32).astype(jnp.bfloat16)
        rounded = lax.optimization_barrier(rounded)
        bounds = np.cumsum([0] + [weight.shape[1] for weight in weights])
        return [
            heads_split(rounded[:, bounds[n] : bounds[n + 1]], width)
            for n, width in enumerate(widths)
        ]

    feat_k_bf, value_bf = project((w_feat_k, w_value), (FEAT, HEAD_DIM))
    feat_q_bf, query_bf, key_all_bf = project((w_feat_q, w_query, w_key), (FEAT, HEAD_DIM, HEAD_DIM))
    feat_q = feat_q_bf.astype(jnp.float32)
    feat_k = feat_k_bf.astype(jnp.float32)
    value = value_bf.astype(jnp.float32)
    head_width = w_query.shape[1]
    rows_here = segment.shape[0]
    key_tail_bf = key_all_bf[:, -WINDOW:]
    value_tail_bf = value_bf[:, -WINDOW:]
    seg_mark = jnp.broadcast_to(
        (segment[-WINDOW:] + 1).astype(jnp.bfloat16)[None, :, None], (key_tail_bf.shape[0], WINDOW, HEAD_DIM)
    )
    tails = passed_along(jnp.concatenate([key_tail_bf, value_tail_bf, seg_mark[:1]], axis=0), "ctx", 1)
    heads_n = key_tail_bf.shape[0]
    tail_key, tail_value = tails[:heads_n], tails[heads_n : 2 * heads_n]
    tail_mark = tails[2 * heads_n, :, 0]
    mapped_k = taylor_map(feat_k) * (segment == segment[-1])[None, :, None].astype(jnp.float32)
    own_state = jnp.einsum("htf,htd->hfd", mapped_k, value, precision=HIGH)
    own_normal = jnp.sum(mapped_k, axis=1)
    carried_state, carried_normal, carried_last = carried_in(
        own_state, own_normal, segment[-1:], "ctx", FEAT
    )
    seg_float = segment.astype(jnp.float32)
    key_rows = jnp.concatenate([tail_key, key_all_bf], axis=1)
    value_rows = jnp.concatenate([tail_value.astype(jnp.float32), value], axis=1)
    key_seg = jnp.concatenate([tail_mark.astype(jnp.float32), seg_float + 1.0])
    owners = lax.axis_size("tp")
    own = rows_here // owners
    bounds = (0, own // 4, own)
    heads = feat_q.shape[0]

    def pick(array, j):
        shape = array.shape
        grouped = array.reshape(shape[:-2] + (owners, own, shape[-1]))
        taken = grouped[..., bounds[j] : bounds[j + 1], :]
        return taken.reshape(shape[:-2] + (owners * (bounds[j + 1] - bounds[j]), shape[-1]))

    keep, _ = fold_pairs(FEAT)
    doubled = np.concatenate(
        [np.ones(1 + FEAT), [1.0 if i == j else 2.0 for i in range(FEAT) for j in range(i, FEAT)]]
    ).astype(np.float32)
    pieces = []
    for j in range(len(bounds) - 1):
        sub = bounds[j + 1] - bounds[j]
        local = np.arange(sub)
        reach = np.arange(sub + WINDOW)
        near = (reach[None, :] <= local[:, None] + WINDOW) & (reach[None, :] > local[:, None])
        query_pos = (np.arange(owners)[:, None] * own + bounds[j] + local[None, :]).reshape(-1)
        key_pos = np.arange(rows_here)
        seg_here = seg_float.reshape(owners, own)[:, bounds[j] : bounds[j + 1]].reshape(-1)
        allowed = (seg_here[:, None] == seg_float[None, :]) & (key_pos[None, :] <= query_pos[:, None])
        inner = (
            jnp.einsum(
                "hsf,htf->hst",
                pick(feat_q_bf, j),
                feat_k_bf,
                preferred_element_type=jnp.float32,
            )
            / FEAT**0.5
        )
        kernel = jnp.where(allowed[None], 1.0 + inner + 0.5 * inner * inner, 0.0)
        numerator = jnp.einsum("hst,htd->hsd", kernel, value, precision=HIGH)
        denominator = jnp.sum(kernel, axis=-1)
        mapped_q = jnp.take(taylor_map(pick(feat_q, j)), keep, axis=-1) * doubled
        carried = (seg_here == carried_last)[None, :]
        numerator = numerator + jnp.where(
            carried[..., None],
            jnp.einsum("hsf,hfd->hsd", mapped_q, carried_state, precision=HIGH),
            0.0,
        )
        denominator = denominator + jnp.where(
            carried, jnp.einsum("hsf,hf->hs", mapped_q, carried_normal, precision=HIGH), 0.0
        )
        linear_part = numerator / denominator[..., None]
        starts = [b * own + bounds[j] for b in range(owners)]
        key_blocks = jnp.stack([key_rows[:, s : s + sub + WINDOW] for s in starts], axis=1)
        value_blocks = jnp.stack([value_rows[:, s : s + sub + WINDOW] for s in starts], axis=1)
        seg_blocks = jnp.stack([key_seg[s : s + sub + WINDOW] for s in starts], axis=0)
        query_blocks = pick(query_bf, j).reshape(heads, owners, sub, HEAD_DIM)
        visible = near[None] & (seg_blocks[:, None, :] == seg_here.reshape(owners, sub)[:, :, None] + 1.0)
        scores = (
            jnp.einsum(
                "hbsd,hbtd->hbst",
                query_blocks,
                key_blocks,
                preferred_element_type=jnp.float32,
            )
            / HEAD_DIM**0.5
        )
        scores = jnp.where(visible[None], scores, -jnp.inf)
        peak = jnp.max(scores, axis=-1, keepdims=True)
        expo = jnp.exp(scores - peak)
        window_part = (
            jnp.einsum("hbst,hbtd->hbsd", expo, value_blocks, precision=HIGH)
            / jnp.sum(expo, axis=-1)[..., None]
        ).reshape(heads, owners * sub, HEAD_DIM)
        mixed = (
            (linear_part + window_part)
            .transpose(1, 0, 2)
            .reshape(owners * sub, head_width)
            .astype(jnp.bfloat16)
        )
        pieces.append(
            lax.psum_scatter(
                jnp.dot(mixed, w_out, preferred_element_type=jnp.float32),
                "tp",
                scatter_dimension=0,
                tiled=True,
            ).astype(jnp.bfloat16)
        )
    return jnp.concatenate(pieces, axis=0)


def solution(mesh):
    in_specs = (
        P(("ctx", "tp"), None),
        P("ctx"),
        P(None, "tp"),
        P(None, "tp"),
        P(None, "tp"),
        P(None, "tp"),
        P(None, "tp"),
        P("tp", None),
    )
    out_specs = P(("ctx", "tp"), None)
    return jax.shard_map(body, mesh=mesh, in_specs=in_specs, out_specs=out_specs, check_vma=False)
```

```python
import jax
import numpy as np
import jax.numpy as jnp
from jax import lax
from jax.sharding import PartitionSpec as P

HEAD_DIM = 128
FEAT = 16
WINDOW = 64


HIGH = lax.Precision.HIGH


def passed_along(block, axis, distance):
    devices = range(lax.axis_size(axis))
    route = [(i - distance, i) for i in devices if i - distance in devices]
    return lax.ppermute(block, axis, route)


def fold_pairs(width):
    upper = [i * width + j for i in range(width) for j in range(i, width)]
    place = {pair: n for n, pair in enumerate(upper)}
    full = [place[min(i, j) * width + max(i, j)] for i in range(width) for j in range(width)]
    keep = np.concatenate([np.arange(1 + width), 1 + width + np.array(upper)])
    back = np.concatenate([np.arange(1 + width), 1 + width + np.array(full)])
    return keep, back


def carried_in(state, normal, last, axis, width):
    place = lax.axis_index(axis)
    length = lax.axis_size(axis)
    keep, back = fold_pairs(width)
    state = jnp.take(state, keep, axis=1)
    normal = jnp.take(normal, keep, axis=1)
    heads, features, lanes = state.shape
    extra = -(-(features + 1) // lanes)
    row, column = features + features // lanes, features % lanes
    tagged = jnp.concatenate(
        [normal, jnp.broadcast_to(last.astype(jnp.float32)[0], (heads, 1))], axis=1
    )
    tagged = jnp.pad(tagged, ((0, 0), (0, extra * lanes - features - 1)))
    packed = jnp.concatenate([state, tagged.reshape(heads, extra, lanes)], axis=1)
    everything = lax.all_gather(packed, axis)
    tags = everything[:, 0, row, column]
    order = jnp.arange(length)
    before_tag = jnp.sum(jnp.where(order == place - 1, tags, 0.0))
    before_tag = jnp.where(place >= 1, before_tag, -1.0)
    chosen = (order < place) & (tags == before_tag)
    before = jnp.sum(jnp.where(chosen[:, None, None, None], everything, 0.0), axis=0)
    flat = before[:, features:].reshape(heads, extra * lanes)
    return (
        jnp.take(before[:, :features], back, axis=1),
        jnp.take(flat[:, :features], back, axis=1),
        before_tag,
    )


def taylor_map(values):
    width = values.shape[-1]
    square = (values[..., :, None] * values[..., None, :]).reshape(
        values.shape[:-1] + (width * width,)
    )
    ones = jnp.ones(values.shape[:-1] + (1,), values.dtype)
    return jnp.concatenate(
        [ones, values * width ** (-0.25), square * (0.5**0.5 / width**0.5)], axis=-1
    )


def heads_split(flat, width):
    return flat.reshape(flat.shape[0], -1, width).transpose(1, 0, 2)


def body(tokens, segment, w_feat_q, w_feat_k, w_query, w_key, w_value, w_out):
    piece = lax.all_gather(tokens, "tp", axis=0, tiled=True)

    def project(weights, widths):
        joined = jnp.concatenate(weights, axis=1)
        rounded = jnp.dot(piece, joined, preferred_element_type=jnp.float32).astype(jnp.bfloat16)
        rounded = lax.optimization_barrier(rounded)
        bounds = np.cumsum([0] + [weight.shape[1] for weight in weights])
        return [
            heads_split(rounded[:, bounds[n] : bounds[n + 1]], width)
            for n, width in enumerate(widths)
        ]

    feat_k_bf, value_bf = project((w_feat_k, w_value), (FEAT, HEAD_DIM))
    feat_q_bf, query_bf, key_all_bf = project((w_feat_q, w_query, w_key), (FEAT, HEAD_DIM, HEAD_DIM))
    feat_q = feat_q_bf.astype(jnp.float32)
    feat_k = feat_k_bf.astype(jnp.float32)
    value = value_bf.astype(jnp.float32)
    head_width = w_query.shape[1]
    rows_here = segment.shape[0]
    key_tail_bf = key_all_bf[:, -WINDOW:]
    value_tail_bf = value_bf[:, -WINDOW:]
    seg_mark = jnp.broadcast_to(
        (segment[-WINDOW:] + 1).astype(jnp.bfloat16)[None, :, None], (key_tail_bf.shape[0], WINDOW, HEAD_DIM)
    )
    tails = passed_along(jnp.concatenate([key_tail_bf, value_tail_bf, seg_mark[:1]], axis=0), "ctx", 1)
    heads_n = key_tail_bf.shape[0]
    tail_key, tail_value = tails[:heads_n], tails[heads_n : 2 * heads_n]
    tail_mark = tails[2 * heads_n, :, 0]
    mapped_k = taylor_map(feat_k) * (segment == segment[-1])[None, :, None].astype(jnp.float32)
    own_state = jnp.einsum("htf,htd->hfd", mapped_k, value, precision=HIGH)
    own_normal = jnp.sum(mapped_k, axis=1)
    carried_state, carried_normal, carried_last = carried_in(
        own_state, own_normal, segment[-1:], "ctx", FEAT
    )
    seg_float = segment.astype(jnp.float32)
    key_rows = jnp.concatenate([tail_key, key_all_bf], axis=1)
    value_rows = jnp.concatenate([tail_value.astype(jnp.float32), value], axis=1)
    key_seg = jnp.concatenate([tail_mark.astype(jnp.float32), seg_float + 1.0])
    owners = lax.axis_size("tp")
    own = rows_here // owners
    bounds = (0, own // 4, own)
    heads = feat_q.shape[0]

    def pick(array, j):
        shape = array.shape
        grouped = array.reshape(shape[:-2] + (owners, own, shape[-1]))
        taken = grouped[..., bounds[j] : bounds[j + 1], :]
        return taken.reshape(shape[:-2] + (owners * (bounds[j + 1] - bounds[j]), shape[-1]))

    pieces = []
    for j in range(len(bounds) - 1):
        sub = bounds[j + 1] - bounds[j]
        local = np.arange(sub)
        reach = np.arange(sub + WINDOW)
        near = (reach[None, :] <= local[:, None] + WINDOW) & (reach[None, :] > local[:, None])
        query_pos = (np.arange(owners)[:, None] * own + bounds[j] + local[None, :]).reshape(-1)
        key_pos = np.arange(rows_here)
        seg_here = seg_float.reshape(owners, own)[:, bounds[j] : bounds[j + 1]].reshape(-1)
        allowed = (seg_here[:, None] == seg_float[None, :]) & (key_pos[None, :] <= query_pos[:, None])
        inner = (
            jnp.einsum(
                "hsf,htf->hst",
                pick(feat_q_bf, j),
                feat_k_bf,
                preferred_element_type=jnp.float32,
            )
            / FEAT**0.5
        )
        kernel = jnp.where(allowed[None], 1.0 + inner + 0.5 * inner * inner, 0.0)
        numerator = jnp.einsum("hst,htd->hsd", kernel, value, preferred_element_type=jnp.float32)
        denominator = jnp.sum(kernel, axis=-1)
        mapped_q = taylor_map(pick(feat_q, j))
        carried = (seg_here == carried_last)[None, :]
        numerator = numerator + jnp.where(
            carried[..., None],
            jnp.einsum("hsf,hfd->hsd", mapped_q, carried_state, precision=HIGH),
            0.0,
        )
        denominator = denominator + jnp.where(
            carried, jnp.einsum("hsf,hf->hs", mapped_q, carried_normal, precision=HIGH), 0.0
        )
        linear_part = numerator / denominator[..., None]
        starts = [b * own + bounds[j] for b in range(owners)]
        key_blocks = jnp.stack([key_rows[:, s : s + sub + WINDOW] for s in starts], axis=1)
        value_blocks = jnp.stack([value_rows[:, s : s + sub + WINDOW] for s in starts], axis=1)
        seg_blocks = jnp.stack([key_seg[s : s + sub + WINDOW] for s in starts], axis=0)
        query_blocks = pick(query_bf, j).reshape(heads, owners, sub, HEAD_DIM)
        visible = near[None] & (seg_blocks[:, None, :] == seg_here.reshape(owners, sub)[:, :, None] + 1.0)
        scores = (
            jnp.einsum(
                "hbsd,hbtd->hbst",
                query_blocks,
                key_blocks,
                preferred_element_type=jnp.float32,
            )
            / HEAD_DIM**0.5
        )
        scores = jnp.where(visible[None], scores, -jnp.inf)
        peak = jnp.max(scores, axis=-1, keepdims=True)
        expo = jnp.exp(scores - peak)
        window_part = (
            jnp.einsum("hbst,hbtd->hbsd", expo, value_blocks, preferred_element_type=jnp.float32)
            / jnp.sum(expo, axis=-1)[..., None]
        ).reshape(heads, owners * sub, HEAD_DIM)
        mixed = (
            (linear_part + window_part)
            .transpose(1, 0, 2)
            .reshape(owners * sub, head_width)
            .astype(jnp.bfloat16)
        )
        pieces.append(
            lax.psum_scatter(
                jnp.dot(mixed, w_out, preferred_element_type=jnp.float32),
                "tp",
                scatter_dimension=0,
                tiled=True,
            ).astype(jnp.bfloat16)
        )
    return jnp.concatenate(pieces, axis=0)


def solution(mesh):
    in_specs = (
        P(("ctx", "tp"), None),
        P("ctx"),
        P(None, "tp"),
        P(None, "tp"),
        P(None, "tp"),
        P(None, "tp"),
        P(None, "tp"),
        P("tp", None),
    )
    out_specs = P(("ctx", "tp"), None)
    return jax.shard_map(body, mesh=mesh, in_specs=in_specs, out_specs=out_specs, check_vma=False)
```

```python
import jax
import numpy as np
import jax.numpy as jnp
from jax import lax
from jax.sharding import PartitionSpec as P

HEAD_DIM = 128
FEAT = 16
WINDOW = 64


HIGH = lax.Precision.HIGH


def passed_along(block, axis, distance):
    devices = range(lax.axis_size(axis))
    route = [(i - distance, i) for i in devices if i - distance in devices]
    return lax.ppermute(block, axis, route)


def fold_pairs(width):
    upper = [i * width + j for i in range(width) for j in range(i, width)]
    place = {pair: n for n, pair in enumerate(upper)}
    full = [place[min(i, j) * width + max(i, j)] for i in range(width) for j in range(width)]
    keep = np.concatenate([np.arange(1 + width), 1 + width + np.array(upper)])
    back = np.concatenate([np.arange(1 + width), 1 + width + np.array(full)])
    return keep, back


def carried_in(state, normal, last, axis, width):
    place = lax.axis_index(axis)
    length = lax.axis_size(axis)
    keep, back = fold_pairs(width)
    state = jnp.take(state, keep, axis=1)
    normal = jnp.take(normal, keep, axis=1)
    heads, features, lanes = state.shape
    extra = -(-(features + 1) // lanes)
    row, column = features + features // lanes, features % lanes
    tagged = jnp.concatenate(
        [normal, jnp.broadcast_to(last.astype(jnp.float32)[0], (heads, 1))], axis=1
    )
    tagged = jnp.pad(tagged, ((0, 0), (0, extra * lanes - features - 1)))
    packed = jnp.concatenate([state, tagged.reshape(heads, extra, lanes)], axis=1)
    everything = lax.all_gather(packed, axis)
    tags = everything[:, 0, row, column]
    order = jnp.arange(length)
    before_tag = jnp.sum(jnp.where(order == place - 1, tags, 0.0))
    before_tag = jnp.where(place >= 1, before_tag, -1.0)
    chosen = (order < place) & (tags == before_tag)
    before = jnp.sum(jnp.where(chosen[:, None, None, None], everything, 0.0), axis=0)
    flat = before[:, features:].reshape(heads, extra * lanes)
    return (
        jnp.take(before[:, :features], back, axis=1),
        jnp.take(flat[:, :features], back, axis=1),
        before_tag,
    )


def taylor_map(values):
    width = values.shape[-1]
    square = (values[..., :, None] * values[..., None, :]).reshape(
        values.shape[:-1] + (width * width,)
    )
    ones = jnp.ones(values.shape[:-1] + (1,), values.dtype)
    return jnp.concatenate(
        [ones, values * width ** (-0.25), square * (0.5**0.5 / width**0.5)], axis=-1
    )


def heads_split(flat, width):
    return flat.reshape(flat.shape[0], -1, width).transpose(1, 0, 2)


def body(tokens, segment, w_feat_q, w_feat_k, w_query, w_key, w_value, w_out):
    piece = lax.all_gather(tokens, "tp", axis=0, tiled=True)

    def project(weights, widths):
        joined = jnp.concatenate(weights, axis=1)
        rounded = jnp.dot(piece, joined, preferred_element_type=jnp.float32).astype(jnp.bfloat16)
        rounded = lax.optimization_barrier(rounded)
        bounds = np.cumsum([0] + [weight.shape[1] for weight in weights])
        return [
            heads_split(rounded[:, bounds[n] : bounds[n + 1]], width)
            for n, width in enumerate(widths)
        ]

    feat_k_bf, value_bf = project((w_feat_k, w_value), (FEAT, HEAD_DIM))
    feat_q_bf, query_bf, key_all_bf = project((w_feat_q, w_query, w_key), (FEAT, HEAD_DIM, HEAD_DIM))
    feat_q = feat_q_bf.astype(jnp.float32)
    feat_k = feat_k_bf.astype(jnp.float32)
    value = value_bf.astype(jnp.float32)
    head_width = w_query.shape[1]
    rows_here = segment.shape[0]
    key_tail_bf = key_all_bf[:, -WINDOW:]
    value_tail_bf = value_bf[:, -WINDOW:]
    seg_mark = jnp.broadcast_to(
        (segment[-WINDOW:] + 1).astype(jnp.bfloat16)[None, :, None], (key_tail_bf.shape[0], WINDOW, HEAD_DIM)
    )
    tails = passed_along(jnp.concatenate([key_tail_bf, value_tail_bf, seg_mark[:1]], axis=0), "ctx", 1)
    heads_n = key_tail_bf.shape[0]
    tail_key, tail_value = tails[:heads_n], tails[heads_n : 2 * heads_n]
    tail_mark = tails[2 * heads_n, :, 0]
    mapped_k = taylor_map(feat_k) * (segment == segment[-1])[None, :, None].astype(jnp.float32)
    own_state = jnp.einsum("htf,htd->hfd", mapped_k, value, precision=HIGH)
    own_normal = jnp.sum(mapped_k, axis=1)
    carried_state, carried_normal, carried_last = carried_in(
        own_state, own_normal, segment[-1:], "ctx", FEAT
    )
    seg_float = segment.astype(jnp.float32)
    key_rows = jnp.concatenate([tail_key, key_all_bf], axis=1)
    value_rows = jnp.concatenate([tail_value.astype(jnp.float32), value], axis=1)
    key_seg = jnp.concatenate([tail_mark.astype(jnp.float32), seg_float + 1.0])
    owners = lax.axis_size("tp")
    own = rows_here // owners
    bounds = (0, own * 5 // 16, own)
    heads = feat_q.shape[0]

    def pick(array, j):
        shape = array.shape
        grouped = array.reshape(shape[:-2] + (owners, own, shape[-1]))
        taken = grouped[..., bounds[j] : bounds[j + 1], :]
        return taken.reshape(shape[:-2] + (owners * (bounds[j + 1] - bounds[j]), shape[-1]))

    pieces = []
    for j in range(len(bounds) - 1):
        sub = bounds[j + 1] - bounds[j]
        local = np.arange(sub)
        reach = np.arange(sub + WINDOW)
        near = (reach[None, :] <= local[:, None] + WINDOW) & (reach[None, :] > local[:, None])
        query_pos = (np.arange(owners)[:, None] * own + bounds[j] + local[None, :]).reshape(-1)
        key_pos = np.arange(rows_here)
        seg_here = seg_float.reshape(owners, own)[:, bounds[j] : bounds[j + 1]].reshape(-1)
        allowed = (seg_here[:, None] == seg_float[None, :]) & (key_pos[None, :] <= query_pos[:, None])
        inner = (
            jnp.einsum(
                "hsf,htf->hst",
                pick(feat_q_bf, j),
                feat_k_bf,
                preferred_element_type=jnp.float32,
            )
            / FEAT**0.5
        )
        kernel = jnp.where(allowed[None], 1.0 + inner + 0.5 * inner * inner, 0.0)
        numerator = jnp.einsum("hst,htd->hsd", kernel, value, precision=HIGH)
        denominator = jnp.sum(kernel, axis=-1)
        mapped_q = taylor_map(pick(feat_q, j))
        carried = (seg_here == carried_last)[None, :]
        numerator = numerator + jnp.where(
            carried[..., None],
            jnp.einsum("hsf,hfd->hsd", mapped_q, carried_state, precision=HIGH),
            0.0,
        )
        denominator = denominator + jnp.where(
            carried, jnp.einsum("hsf,hf->hs", mapped_q, carried_normal, precision=HIGH), 0.0
        )
        linear_part = numerator / denominator[..., None]
        starts = [b * own + bounds[j] for b in range(owners)]
        key_blocks = jnp.stack([key_rows[:, s : s + sub + WINDOW] for s in starts], axis=1)
        value_blocks = jnp.stack([value_rows[:, s : s + sub + WINDOW] for s in starts], axis=1)
        seg_blocks = jnp.stack([key_seg[s : s + sub + WINDOW] for s in starts], axis=0)
        query_blocks = pick(query_bf, j).reshape(heads, owners, sub, HEAD_DIM)
        visible = near[None] & (seg_blocks[:, None, :] == seg_here.reshape(owners, sub)[:, :, None] + 1.0)
        scores = (
            jnp.einsum(
                "hbsd,hbtd->hbst",
                query_blocks,
                key_blocks,
                preferred_element_type=jnp.float32,
            )
            / HEAD_DIM**0.5
        )
        scores = jnp.where(visible[None], scores, -jnp.inf)
        peak = jnp.max(scores, axis=-1, keepdims=True)
        expo = jnp.exp(scores - peak)
        window_part = (
            jnp.einsum("hbst,hbtd->hbsd", expo, value_blocks, precision=HIGH)
            / jnp.sum(expo, axis=-1)[..., None]
        ).reshape(heads, owners * sub, HEAD_DIM)
        mixed = (
            (linear_part + window_part)
            .transpose(1, 0, 2)
            .reshape(owners * sub, head_width)
            .astype(jnp.bfloat16)
        )
        pieces.append(
            lax.psum_scatter(
                jnp.dot(mixed, w_out, preferred_element_type=jnp.float32),
                "tp",
                scatter_dimension=0,
                tiled=True,
            ).astype(jnp.bfloat16)
        )
    return jnp.concatenate(pieces, axis=0)


def solution(mesh):
    in_specs = (
        P(("ctx", "tp"), None),
        P("ctx"),
        P(None, "tp"),
        P(None, "tp"),
        P(None, "tp"),
        P(None, "tp"),
        P(None, "tp"),
        P("tp", None),
    )
    out_specs = P(("ctx", "tp"), None)
    return jax.shard_map(body, mesh=mesh, in_specs=in_specs, out_specs=out_specs, check_vma=False)
```

```python
import jax
import numpy as np
import jax.numpy as jnp
from jax import lax
from jax.sharding import PartitionSpec as P

HEAD_DIM = 128
FEAT = 16
WINDOW = 64


HIGH = lax.Precision.HIGH


def passed_along(block, axis, distance):
    devices = range(lax.axis_size(axis))
    route = [(i - distance, i) for i in devices if i - distance in devices]
    return lax.ppermute(block, axis, route)


def fold_pairs(width):
    upper = [i * width + j for i in range(width) for j in range(i, width)]
    place = {pair: n for n, pair in enumerate(upper)}
    full = [place[min(i, j) * width + max(i, j)] for i in range(width) for j in range(width)]
    keep = np.concatenate([np.arange(1 + width), 1 + width + np.array(upper)])
    back = np.concatenate([np.arange(1 + width), 1 + width + np.array(full)])
    return keep, back


def carried_in(state, normal, last, axis, width):
    place = lax.axis_index(axis)
    length = lax.axis_size(axis)
    keep, back = fold_pairs(width)
    state = jnp.take(state, keep, axis=1)
    normal = jnp.take(normal, keep, axis=1)
    heads, features, lanes = state.shape
    extra = -(-(features + 1) // lanes)
    row, column = features + features // lanes, features % lanes
    tagged = jnp.concatenate(
        [normal, jnp.broadcast_to(last.astype(jnp.float32)[0], (heads, 1))], axis=1
    )
    tagged = jnp.pad(tagged, ((0, 0), (0, extra * lanes - features - 1)))
    packed = jnp.concatenate([state, tagged.reshape(heads, extra, lanes)], axis=1)
    everything = lax.all_gather(packed, axis)
    tags = everything[:, 0, row, column]
    order = jnp.arange(length)
    before_tag = jnp.sum(jnp.where(order == place - 1, tags, 0.0))
    before_tag = jnp.where(place >= 1, before_tag, -1.0)
    chosen = (order < place) & (tags == before_tag)
    before = jnp.sum(jnp.where(chosen[:, None, None, None], everything, 0.0), axis=0)
    flat = before[:, features:].reshape(heads, extra * lanes)
    return (
        jnp.take(before[:, :features], back, axis=1),
        jnp.take(flat[:, :features], back, axis=1),
        before_tag,
    )


def taylor_map(values):
    width = values.shape[-1]
    square = (values[..., :, None] * values[..., None, :]).reshape(
        values.shape[:-1] + (width * width,)
    )
    ones = jnp.ones(values.shape[:-1] + (1,), values.dtype)
    return jnp.concatenate(
        [ones, values * width ** (-0.25), square * (0.5**0.5 / width**0.5)], axis=-1
    )


def heads_split(flat, width):
    return flat.reshape(flat.shape[0], -1, width).transpose(1, 0, 2)


def body(tokens, segment, w_feat_q, w_feat_k, w_query, w_key, w_value, w_out):
    piece = lax.all_gather(tokens, "tp", axis=0, tiled=True)

    def project(weights, widths):
        joined = jnp.concatenate(weights, axis=1)
        rounded = jnp.dot(piece, joined, preferred_element_type=jnp.float32).astype(jnp.bfloat16)
        rounded = lax.optimization_barrier(rounded)
        bounds = np.cumsum([0] + [weight.shape[1] for weight in weights])
        return [
            heads_split(rounded[:, bounds[n] : bounds[n + 1]], width)
            for n, width in enumerate(widths)
        ]

    feat_k_bf, value_bf = project((w_feat_k, w_value), (FEAT, HEAD_DIM))
    feat_q_bf, query_bf, key_all_bf = project((w_feat_q, w_query, w_key), (FEAT, HEAD_DIM, HEAD_DIM))
    feat_q = feat_q_bf.astype(jnp.float32)
    feat_k = feat_k_bf.astype(jnp.float32)
    value = value_bf.astype(jnp.float32)
    head_width = w_query.shape[1]
    rows_here = segment.shape[0]
    key_tail_bf = key_all_bf[:, -WINDOW:]
    value_tail_bf = value_bf[:, -WINDOW:]
    seg_mark = jnp.broadcast_to(
        (segment[-WINDOW:] + 1).astype(jnp.bfloat16)[None, :, None], (key_tail_bf.shape[0], WINDOW, HEAD_DIM)
    )
    tails = passed_along(jnp.concatenate([key_tail_bf, value_tail_bf, seg_mark[:1]], axis=0), "ctx", 1)
    heads_n = key_tail_bf.shape[0]
    tail_key, tail_value = tails[:heads_n], tails[heads_n : 2 * heads_n]
    tail_mark = tails[2 * heads_n, :, 0]
    mapped_k = taylor_map(feat_k) * (segment == segment[-1])[None, :, None].astype(jnp.float32)
    own_state = jnp.einsum("htf,htd->hfd", mapped_k, value, precision=HIGH)
    own_normal = jnp.sum(mapped_k, axis=1)
    carried_state, carried_normal, carried_last = carried_in(
        own_state, own_normal, segment[-1:], "ctx", FEAT
    )
    seg_float = segment.astype(jnp.float32)
    key_rows = jnp.concatenate([tail_key, key_all_bf], axis=1)
    value_rows = jnp.concatenate([tail_value.astype(jnp.float32), value], axis=1)
    key_seg = jnp.concatenate([tail_mark.astype(jnp.float32), seg_float + 1.0])
    owners = lax.axis_size("tp")
    own = rows_here // owners
    bounds = (0, own * 3 // 16, own)
    heads = feat_q.shape[0]

    def pick(array, j):
        shape = array.shape
        grouped = array.reshape(shape[:-2] + (owners, own, shape[-1]))
        taken = grouped[..., bounds[j] : bounds[j + 1], :]
        return taken.reshape(shape[:-2] + (owners * (bounds[j + 1] - bounds[j]), shape[-1]))

    pieces = []
    for j in range(len(bounds) - 1):
        sub = bounds[j + 1] - bounds[j]
        local = np.arange(sub)
        reach = np.arange(sub + WINDOW)
        near = (reach[None, :] <= local[:, None] + WINDOW) & (reach[None, :] > local[:, None])
        query_pos = (np.arange(owners)[:, None] * own + bounds[j] + local[None, :]).reshape(-1)
        key_pos = np.arange(rows_here)
        seg_here = seg_float.reshape(owners, own)[:, bounds[j] : bounds[j + 1]].reshape(-1)
        allowed = (seg_here[:, None] == seg_float[None, :]) & (key_pos[None, :] <= query_pos[:, None])
        inner = (
            jnp.einsum(
                "hsf,htf->hst",
                pick(feat_q_bf, j),
                feat_k_bf,
                preferred_element_type=jnp.float32,
            )
            / FEAT**0.5
        )
        kernel = jnp.where(allowed[None], 1.0 + inner + 0.5 * inner * inner, 0.0)
        numerator = jnp.einsum("hst,htd->hsd", kernel, value, precision=HIGH)
        denominator = jnp.sum(kernel, axis=-1)
        mapped_q = taylor_map(pick(feat_q, j))
        carried = (seg_here == carried_last)[None, :]
        numerator = numerator + jnp.where(
            carried[..., None],
            jnp.einsum("hsf,hfd->hsd", mapped_q, carried_state, precision=HIGH),
            0.0,
        )
        denominator = denominator + jnp.where(
            carried, jnp.einsum("hsf,hf->hs", mapped_q, carried_normal, precision=HIGH), 0.0
        )
        linear_part = numerator / denominator[..., None]
        starts = [b * own + bounds[j] for b in range(owners)]
        key_blocks = jnp.stack([key_rows[:, s : s + sub + WINDOW] for s in starts], axis=1)
        value_blocks = jnp.stack([value_rows[:, s : s + sub + WINDOW] for s in starts], axis=1)
        seg_blocks = jnp.stack([key_seg[s : s + sub + WINDOW] for s in starts], axis=0)
        query_blocks = pick(query_bf, j).reshape(heads, owners, sub, HEAD_DIM)
        visible = near[None] & (seg_blocks[:, None, :] == seg_here.reshape(owners, sub)[:, :, None] + 1.0)
        scores = (
            jnp.einsum(
                "hbsd,hbtd->hbst",
                query_blocks,
                key_blocks,
                preferred_element_type=jnp.float32,
            )
            / HEAD_DIM**0.5
        )
        scores = jnp.where(visible[None], scores, -jnp.inf)
        peak = jnp.max(scores, axis=-1, keepdims=True)
        expo = jnp.exp(scores - peak)
        window_part = (
            jnp.einsum("hbst,hbtd->hbsd", expo, value_blocks, precision=HIGH)
            / jnp.sum(expo, axis=-1)[..., None]
        ).reshape(heads, owners * sub, HEAD_DIM)
        mixed = (
            (linear_part + window_part)
            .transpose(1, 0, 2)
            .reshape(owners * sub, head_width)
            .astype(jnp.bfloat16)
        )
        pieces.append(
            lax.psum_scatter(
                jnp.dot(mixed, w_out, preferred_element_type=jnp.float32),
                "tp",
                scatter_dimension=0,
                tiled=True,
            ).astype(jnp.bfloat16)
        )
    return jnp.concatenate(pieces, axis=0)


def solution(mesh):
    in_specs = (
        P(("ctx", "tp"), None),
        P("ctx"),
        P(None, "tp"),
        P(None, "tp"),
        P(None, "tp"),
        P(None, "tp"),
        P(None, "tp"),
        P("tp", None),
    )
    out_specs = P(("ctx", "tp"), None)
    return jax.shard_map(body, mesh=mesh, in_specs=in_specs, out_specs=out_specs, check_vma=False)
```
